256 devices in a mesh: dp: 4 (over y), seq: 64 (over z, x, core).
Axes of the slice: x: 4, y: 4, z: 8, core: 2. Of those that a mesh axis runs over, the one named last changes fastest.
Arguments:
- features: bfloat16 [49152, 1408], P(('dp', 'seq')), parts along dimension 0, may hold values from -6 to 6
- norm_gain: float32 [1408], replicated, may hold values from 0.1 to 1.9
- conv_weight: bfloat16 [5, 1408, 1536], P(None, None, 'seq'), may hold values from -0.0625 to 0.0625
- conv_bias: float32 [1536], replicated, may hold values from -3 to 3
- attn_gain: float32 [1536], replicated, may hold values from 0.1 to 1.9
- query_weight: bfloat16 [1536, 1024], P('seq'), may hold values from -1 to 1
- keyval_weight: bfloat16 [1536, 256], P('seq'), may hold values from -1 to 1
- head_scale: float32 [8], replicated, may hold values from 1 to 4
- output_weight: bfloat16 [1024, 1536], P('seq'), may hold values from -0.1875 to 0.1875
Outputs:
- coarse: bfloat16 [24576, 1536], P(('dp', 'seq')), parts along dimension 0
- attended: bfloat16 [24576, 1536], P(('dp', 'seq')), parts along dimension 0
The draws below stay inside these ranges and needn't reach their ends.
There are 4 independent parts, one for each index of `dp`. The reference program is written for one: setup_inputs(seed, part) draws one part's arguments, and reference() takes and returns one part's arrays. A program takes and returns all parts, laid end to end along the dimension named above; an argument that names none is the same for every part. Nothing has to cross between parts.
All inputs are finite; a program needn't handle non-finite values.
Results may differ from the reference program's by a relative error of at most 0.007.
Values may be sent and summed in bfloat16 or wider, within the bound.
No kernel may reach another device: no remote copies, remote signals or barrier semaphores. Data moves between devices by JAX's collectives and lax.ppermute only.
A program may use at most 128 MiB of HBM per device.

```python
import math
import jax
import jax.numpy as jnp
from jax import lax

CH_IN = 1408
CH_OUT = 1536
HEADS = 8
HEAD_DIM = 128
KWIDTH = 5
FINE_LEN = 12288


def shared_weights(key):
    base = jax.random.fold_in(key, 11)
    key_query, key_keyval = jax.random.split(base, 2)
    keyvals = jax.random.normal(key_keyval, (CH_OUT, 2 * HEAD_DIM), jnp.float32) * CH_OUT ** (-0.5)
    noise = jax.random.normal(key_query, (CH_OUT, HEADS, HEAD_DIM), jnp.float32) * CH_OUT ** (-0.5)
    queries = noise
    queries = jnp.clip(queries.reshape(CH_OUT, HEADS * HEAD_DIM), -1.0, 1.0)
    return (queries, jnp.clip(keyvals, -1.0, 1.0))


def draw_query_weight(key, part):
    return shared_weights(key)[0].astype(jnp.bfloat16)


def draw_keyval_weight(key, part):
    return shared_weights(key)[1].astype(jnp.bfloat16)


def shard_levels(rng, extent, cuts, low, top_value):
    factor_of, own = 1.0, jax.random.fold_in(rng, 6)
    for position, shards_of in cuts:
        draws = jnp.exp(jax.random.uniform(jax.random.fold_in(own, position), (shards_of,), jnp.float32, low / len(cuts), top_value / len(cuts)))
        factor_of = factor_of * jnp.repeat(draws, extent[position] // shards_of).reshape([-1 if axis == position else 1 for axis in range(len(extent))])
    return factor_of


def gaussian(key, extent, spread, reach, pieces=(), held_as=jnp.bfloat16):
    result = jax.random.normal(key, extent, jnp.float32) * spread
    if len(pieces) > 0:
        result = shard_levels(key, extent, pieces, -0.22, 0.18) * result
    return jnp.clip(result, min=-reach, max=reach).astype(held_as)


def setup_inputs(seed: int = 0, part: int = 0) -> dict:
    splits = jax.random.split(jax.random.key(seed), 10)
    part_splits = jax.random.split(jax.random.fold_in(splits[9], part), 10)
    return {
        "features": gaussian(part_splits[0], (FINE_LEN, CH_IN), 1.0, 6.0, ((0, 64),)),
        "norm_gain": jnp.clip(1.0 + 0.18 * jax.random.normal(splits[1], (CH_IN,), jnp.float32), 0.1, 1.9),
        "conv_weight": gaussian(splits[2], (KWIDTH, CH_IN, CH_OUT), (KWIDTH * CH_IN) ** -0.5, 0.0625, ((2, 64),)),
        "conv_bias": gaussian(splits[3], (CH_OUT,), 0.5, 3.0, (), jnp.float32),
        "attn_gain": jnp.clip(1.0 + 0.18 * jax.random.normal(splits[4], (CH_OUT,), jnp.float32), 0.1, 1.9),
        "query_weight": draw_query_weight(jax.random.fold_in(splits[9], 71), part),
        "keyval_weight": draw_keyval_weight(jax.random.fold_in(splits[9], 71), part),
        "head_scale": jnp.clip(jnp.exp(jax.random.uniform(splits[7], (HEADS,), jnp.float32, math.log(1.0), math.log(4.0))), 1.0, 4.0),
        "output_weight": gaussian(splits[8], (HEADS * HEAD_DIM, CH_OUT), (HEADS * HEAD_DIM) ** -0.5, 0.1875, ((0, 64),)),
    }


def normalize(values_in, channel_gain):
    meansq = lax.optimization_barrier(jnp.mean(values_in * values_in, axis=-1, keepdims=True))
    return values_in * lax.rsqrt(meansq + 1e-06) * channel_gain

def reference(features, norm_gain, conv_weight, conv_bias, attn_gain, query_weight, keyval_weight, head_scale, output_weight):
    normed = jax.nn.gelu(normalize(features.astype(jnp.float32), norm_gain)).astype(jnp.bfloat16)
    row_count = normed.shape[0]
    padded = jnp.pad(normed, ((2, 2), (0, 0)))
    summed = jnp.zeros((row_count, conv_weight.shape[2]), jnp.float32)
    for kernel_tap in range(KWIDTH):
        summed = summed + jnp.dot(padded[kernel_tap:kernel_tap + row_count], conv_weight[kernel_tap], preferred_element_type=jnp.float32)
    levels = summed + conv_bias[None, :]
    coarse = lax.optimization_barrier(jnp.max(levels.reshape(-1, 2, levels.shape[1]), axis=1)).astype(jnp.bfloat16)
    attn_in = normalize(coarse.astype(jnp.float32), attn_gain).astype(jnp.bfloat16)
    queries = jnp.dot(attn_in, query_weight, preferred_element_type=jnp.float32).astype(jnp.bfloat16)
    keyvals = jnp.dot(attn_in, keyval_weight, preferred_element_type=jnp.float32).astype(jnp.bfloat16)
    keys_all = keyvals[:, :HEAD_DIM]
    values_all = keyvals[:, HEAD_DIM:]
    positions = queries.shape[0]
    head_queries = queries.reshape(positions, HEADS, HEAD_DIM).transpose(1, 0, 2)

    def one_head(operands):
        head_query, scale_one = operands
        scores = jnp.dot(head_query, keys_all.T, preferred_element_type=jnp.float32) * scale_one * HEAD_DIM ** (-0.5)
        biggest = lax.optimization_barrier(jnp.max(scores, axis=1, keepdims=True))
        expon = jnp.exp(scores - biggest)
        denom = lax.optimization_barrier(jnp.sum(expon, axis=1, keepdims=True))
        return jnp.dot(expon.astype(jnp.bfloat16), values_all, preferred_element_type=jnp.float32) / denom
    contexts = lax.map(one_head, (head_queries, head_scale))
    context = contexts.transpose(1, 0, 2).reshape(positions, HEADS * HEAD_DIM).astype(jnp.bfloat16)
    attended = jnp.dot(context, output_weight, preferred_element_type=jnp.float32).astype(jnp.bfloat16)
    return (coarse, attended)
```

```python
import jax
import jax.numpy as jnp
from jax import lax
from jax.sharding import Mesh
from jax.sharding import PartitionSpec as P

HEAD_DIM = 128


def normalize(values_in, channel_gain):
    meansq = jnp.mean(values_in * values_in, axis=-1, keepdims=True)
    return values_in * lax.rsqrt(meansq + 1e-06) * channel_gain


def convolve(padded, kernel, row_count):
    summed = jnp.zeros((row_count, kernel.shape[2]), jnp.float32)
    for kernel_tap in range(kernel.shape[0]):
        summed = summed + jnp.dot(
            padded[kernel_tap : kernel_tap + row_count],
            kernel[kernel_tap],
            preferred_element_type=jnp.float32,
        )
    return summed


def pool_pairs(levels):
    return jnp.max(levels.reshape(-1, 2, levels.shape[1]), axis=1)


def gather_rows(block):
    inner = lax.all_gather(block, "sx", axis=0, tiled=True)
    return lax.all_gather(inner, "sz", axis=0, tiled=True)


def attend(queries, key_block, scales):
    row_count = queries.shape[0]
    head_count = scales.shape[0]
    shaped = queries.reshape(row_count, head_count, HEAD_DIM)
    key_part = key_block[:, :HEAD_DIM]
    value_part = key_block[:, HEAD_DIM:]
    scores = (
        jnp.einsum("qhd,kd->hqk", shaped, key_part, preferred_element_type=jnp.float32)
        * scales[:, None, None]
        * HEAD_DIM ** (-0.5)
    )
    biggest = jnp.max(scores, axis=2)
    expon = jnp.exp(scores - biggest[:, :, None])
    total = jnp.sum(expon, axis=2)
    context = jnp.einsum(
        "hqk,kd->hqd", expon.astype(jnp.bfloat16), value_part, preferred_element_type=jnp.float32
    )
    context = context / total[:, :, None]
    return context.transpose(1, 0, 2).reshape(row_count, head_count * HEAD_DIM).astype(jnp.bfloat16)


def shards(
    features,
    norm_gain,
    conv_weight,
    conv_bias,
    attn_gain,
    query_weight,
    keyval_weight,
    head_scale,
    output_weight,
):
    nz = lax.axis_size("sz")
    nx = lax.axis_size("sx")
    me_x = lax.axis_index("sx")
    rows_here = features.shape[0]
    width = conv_weight.shape[2]
    ch_out = conv_bias.shape[0]

    kernel = lax.all_gather(conv_weight, "sz", axis=2, tiled=True)
    proj_weight = gather_rows(jnp.concatenate([query_weight, keyval_weight], axis=1))
    out_weight = gather_rows(output_weight)

    normed = jax.nn.gelu(normalize(features.astype(jnp.float32), norm_gain)).astype(jnp.bfloat16)
    plane = lax.all_gather(normed, "sx", axis=0, tiled=True)
    plane_rows = plane.shape[0]
    forward = [(i, i + 1) for i in range(nz - 1)]
    backward = [(i + 1, i) for i in range(nz - 1)]
    low = lax.ppermute(plane[plane_rows - 2 :], "sz", forward)
    high = lax.ppermute(plane[:2], "sz", backward)
    padded = jnp.concatenate([low, plane, high], axis=0)

    bias_all = conv_bias.reshape(nz, nx, width).transpose(1, 0, 2)
    bias = lax.dynamic_index_in_dim(bias_all, me_x, axis=0, keepdims=False).reshape(nz * width)
    levels = convolve(padded, kernel, plane_rows) + bias[None, :]
    pooled = pool_pairs(levels).astype(jnp.bfloat16)

    coarse_rows = rows_here // 2
    pieces = pooled.reshape(nx, coarse_rows, nz * width)
    received = lax.all_to_all(pieces, "sx", 0, 0, tiled=False)
    coarse = (
        received.reshape(nx, coarse_rows, nz, width)
        .transpose(1, 2, 0, 3)
        .reshape(coarse_rows, ch_out)
    )

    attn_in = normalize(coarse.astype(jnp.float32), attn_gain).astype(jnp.bfloat16)
    proj = jnp.dot(attn_in, proj_weight, preferred_element_type=jnp.float32)
    q_cols = query_weight.shape[1]
    queries = proj[:, :q_cols].astype(jnp.bfloat16)
    keyvals = proj[:, q_cols:].astype(jnp.bfloat16)
    key_block = gather_rows(keyvals)
    context = attend(queries, key_block, head_scale)
    projected = jnp.dot(context, out_weight, preferred_element_type=jnp.float32)
    return (coarse, projected.astype(jnp.bfloat16))


def solution(mesh):
    dp = mesh.shape["dp"]
    seq = mesh.shape["seq"]
    nx = 8 if seq % 8 == 0 else seq
    nz = seq // nx
    grid = Mesh(mesh.devices.reshape(dp, nz, nx), ("dp", "sz", "sx"))
    rows = P(("dp", "sz", "sx"), None)
    return jax.shard_map(
        shards,
        mesh=grid,
        in_specs=(
            rows,
            P(),
            P(None, None, ("sz", "sx")),
            P(),
            P(),
            P(("sz", "sx"), None),
            P(("sz", "sx"), None),
            P(),
            P(("sz", "sx"), None),
        ),
        out_specs=(rows, rows),
        check_vma=False,
    )
```

```python
import jax
import jax.numpy as jnp
from jax import lax
from jax.sharding import Mesh
from jax.sharding import PartitionSpec as P

HEAD_DIM = 128


def normalize(values_in, channel_gain):
    meansq = jnp.mean(values_in * values_in, axis=-1, keepdims=True)
    return values_in * lax.rsqrt(meansq + 1e-06) * channel_gain


def convolve(padded, kernel, row_count):
    summed = jnp.zeros((row_count, kernel.shape[2]), jnp.float32)
    for kernel_tap in range(kernel.shape[0]):
        summed = summed + jnp.dot(
            padded[kernel_tap : kernel_tap + row_count],
            kernel[kernel_tap],
            preferred_element_type=jnp.float32,
        )
    return summed


def pool_pairs(levels):
    return jnp.max(levels.reshape(-1, 2, levels.shape[1]), axis=1)


def spread_in_plane(block):
    inner = lax.all_gather(block, "sxx", axis=0, tiled=True)
    return lax.all_gather(inner, "core", axis=0, tiled=True)


def plane_order(columns, nz, nxx, nc):
    rows = columns.shape[0]
    return (
        columns.reshape(rows, nz, nxx, nc, -1)
        .transpose(0, 3, 2, 1, 4)
        .reshape(rows, columns.shape[1])
    )


def attend(queries, key_block, scales):
    row_count = queries.shape[0]
    head_count = scales.shape[0]
    shaped = queries.reshape(row_count, head_count, HEAD_DIM)
    key_part = key_block[:, :HEAD_DIM]
    value_part = key_block[:, HEAD_DIM:]
    scores = (
        jnp.einsum("qhd,kd->hqk", shaped, key_part, preferred_element_type=jnp.float32)
        * scales[:, None, None]
        * HEAD_DIM ** (-0.5)
    )
    biggest = jnp.max(scores, axis=2)
    expon = jnp.exp(scores - biggest[:, :, None])
    total = jnp.sum(expon, axis=2)
    context = jnp.einsum(
        "hqk,kd->hqd", expon.astype(jnp.bfloat16), value_part, preferred_element_type=jnp.float32
    )
    context = context / total[:, :, None]
    return context.transpose(1, 0, 2).reshape(row_count, head_count * HEAD_DIM).astype(jnp.bfloat16)


def shards(
    features,
    norm_gain,
    conv_weight,
    conv_bias,
    attn_gain,
    query_weight,
    keyval_weight,
    head_scale,
    output_weight,
):
    nz = lax.axis_size("sz")
    nxx = lax.axis_size("sxx")
    nc = lax.axis_size("core")
    nx = nxx * nc
    me_x = lax.axis_index("sxx") * nc + lax.axis_index("core")
    rows_here = features.shape[0]
    taps, ch_in, width = conv_weight.shape
    ch_out = conv_bias.shape[0]

    proj_piece = jnp.concatenate([query_weight, keyval_weight], axis=1)
    pieces = [conv_weight, proj_piece, output_weight]
    sizes = [p.size for p in pieces]
    flat = jnp.concatenate([p.reshape(-1) for p in pieces])
    got = lax.all_gather(flat, "sz", axis=0, tiled=False)
    kernel = (
        got[:, : sizes[0]]
        .reshape(nz, taps, ch_in, width)
        .transpose(1, 2, 0, 3)
        .reshape(taps, ch_in, nz * width)
    )
    proj_z = got[:, sizes[0] : sizes[0] + sizes[1]].reshape(nz * proj_piece.shape[0], proj_piece.shape[1])
    out_z = got[:, sizes[0] + sizes[1] :].reshape(nz * output_weight.shape[0], output_weight.shape[1])

    normed = jax.nn.gelu(normalize(features.astype(jnp.float32), norm_gain)).astype(jnp.bfloat16)
    plane = lax.all_gather(normed, ("sxx", "core"), axis=0, tiled=True)
    plane_rows = plane.shape[0]
    forward = [(i, i + 1) for i in range(nz - 1)]
    backward = [(i + 1, i) for i in range(nz - 1)]
    low = lax.ppermute(plane[plane_rows - 2 :], "sz", forward)
    high = lax.ppermute(plane[:2], "sz", backward)
    padded = jnp.concatenate([low, plane, high], axis=0)

    bias_all = conv_bias.reshape(nz, nx, width).transpose(1, 0, 2)
    bias = lax.dynamic_index_in_dim(bias_all, me_x, axis=0, keepdims=False).reshape(nz * width)
    levels = convolve(padded, kernel, plane_rows) + bias[None, :]
    pooled = pool_pairs(levels).astype(jnp.bfloat16)

    proj_weight = spread_in_plane(proj_z)

    coarse_rows = rows_here // 2
    parts = pooled.reshape(nx, coarse_rows, nz * width)
    received = lax.all_to_all(parts, ("sxx", "core"), 0, 0, tiled=False)
    coarse = (
        received.reshape(nx, coarse_rows, nz, width)
        .transpose(1, 2, 0, 3)
        .reshape(coarse_rows, ch_out)
    )

    attn_in = normalize(coarse.astype(jnp.float32), attn_gain).astype(jnp.bfloat16)
    proj = jnp.dot(plane_order(attn_in, nz, nxx, nc), proj_weight, preferred_element_type=jnp.float32)
    q_cols = query_weight.shape[1]
    queries = proj[:, :q_cols].astype(jnp.bfloat16)
    keyvals = proj[:, q_cols:].astype(jnp.bfloat16)
    key_block = spread_in_plane(lax.all_gather(keyvals, "sz", axis=0, tiled=True))
    out_weight = spread_in_plane(out_z)
    context = attend(queries, key_block, head_scale)
    projected = jnp.dot(plane_order(context, nz, nxx, nc), out_weight, preferred_element_type=jnp.float32)
    return (coarse, projected.astype(jnp.bfloat16))


def solution(mesh):
    dp = mesh.shape["dp"]
    seq = mesh.shape["seq"]
    nc = 2 if seq % 2 == 0 else 1
    nxx = 4 if (seq // nc) % 4 == 0 else seq // nc
    nz = seq // (nc * nxx)
    grid = Mesh(mesh.devices.reshape(dp, nz, nxx, nc), ("dp", "sz", "sxx", "core"))
    seq_axes = ("sz", "sxx", "core")
    rows = P(("dp",) + seq_axes, None)
    return jax.shard_map(
        shards,
        mesh=grid,
        in_specs=(
            rows,
            P(),
            P(None, None, seq_axes),
            P(),
            P(),
            P(seq_axes, None),
            P(seq_axes, None),
            P(),
            P(seq_axes, None),
        ),
        out_specs=(rows, rows),
        check_vma=False,
    )
```

```python
import jax
import jax.numpy as jnp
from jax import lax
from jax.sharding import Mesh
from jax.sharding import PartitionSpec as P

HEAD_DIM = 128


def normalize(values_in, channel_gain):
    meansq = jnp.mean(values_in * values_in, axis=-1, keepdims=True)
    return values_in * lax.rsqrt(meansq + 1e-06) * channel_gain


def convolve(padded, kernel, row_count):
    summed = jnp.zeros((row_count, kernel.shape[2]), jnp.float32)
    for kernel_tap in range(kernel.shape[0]):
        summed = summed + jnp.dot(
            padded[kernel_tap : kernel_tap + row_count],
            kernel[kernel_tap],
            preferred_element_type=jnp.float32,
        )
    return summed


def pool_pairs(levels):
    return jnp.max(levels.reshape(-1, 2, levels.shape[1]), axis=1)


def gather_rows(block):
    inner = lax.all_gather(block, "sx", axis=0, tiled=True)
    return lax.all_gather(inner, "sz", axis=0, tiled=True)


def sx_major(columns, nz, nx):
    rows = columns.shape[0]
    return columns.reshape(rows, nz, nx, -1).transpose(0, 2, 1, 3).reshape(rows, columns.shape[1])


def attend(queries, key_block, scales):
    row_count = queries.shape[0]
    head_count = scales.shape[0]
    shaped = queries.reshape(row_count, head_count, HEAD_DIM)
    key_part = key_block[:, :HEAD_DIM]
    value_part = key_block[:, HEAD_DIM:]
    scores = (
        jnp.einsum("qhd,kd->hqk", shaped, key_part, preferred_element_type=jnp.float32)
        * scales[:, None, None]
        * HEAD_DIM ** (-0.5)
    )
    biggest = jnp.max(scores, axis=2)
    expon = jnp.exp(scores - biggest[:, :, None])
    total = jnp.sum(expon, axis=2)
    context = jnp.einsum(
        "hqk,kd->hqd", expon.astype(jnp.bfloat16), value_part, preferred_element_type=jnp.float32
    )
    context = context / total[:, :, None]
    return context.transpose(1, 0, 2).reshape(row_count, head_count * HEAD_DIM).astype(jnp.bfloat16)


def shards(
    features,
    norm_gain,
    conv_weight,
    conv_bias,
    attn_gain,
    query_weight,
    keyval_weight,
    head_scale,
    output_weight,
):
    nz = lax.axis_size("sz")
    nx = lax.axis_size("sx")
    me_x = lax.axis_index("sx")
    rows_here = features.shape[0]
    width = conv_weight.shape[2]
    ch_out = conv_bias.shape[0]

    me_z = lax.axis_index("sz")
    normed = jax.nn.gelu(normalize(features.astype(jnp.float32), norm_gain)).astype(jnp.bfloat16)
    plane = lax.all_gather(normed, "sx", axis=0, tiled=True)

    slots = [conv_weight]
    for k in range(1, nz):
        slots.append(lax.ppermute(conv_weight, "sz", [(i, (i - k) % nz) for i in range(nz)]))
    kernel = jnp.concatenate(slots, axis=2)

    q_cols = query_weight.shape[1]
    lane = 256
    proj_piece = jnp.concatenate([query_weight, keyval_weight], axis=1)
    proj_n = proj_piece.size // lane
    both = jnp.concatenate(
        [proj_piece.reshape(proj_n, lane), output_weight.reshape(-1, lane)], axis=0
    )
    both_z = lax.all_gather(both, "sz", axis=0, tiled=False)
    proj_z = both_z[:, :proj_n].reshape(nz * proj_piece.shape[0], proj_piece.shape[1])
    out_z = both_z[:, proj_n:].reshape(nz * output_weight.shape[0], output_weight.shape[1])
    proj_weight = lax.all_gather(proj_z, "sx", axis=0, tiled=True)

    plane_rows = plane.shape[0]
    forward = [(i, i + 1) for i in range(nz - 1)]
    backward = [(i + 1, i) for i in range(nz - 1)]
    low = lax.ppermute(plane[plane_rows - 2 :], "sz", forward)
    high = lax.ppermute(plane[:2], "sz", backward)
    padded = jnp.concatenate([low, plane, high], axis=0)

    bias_all = conv_bias.reshape(nz, nx, width).transpose(1, 0, 2)
    bias = lax.dynamic_index_in_dim(bias_all, me_x, axis=0, keepdims=False)
    bias = jnp.roll(bias, -me_z, axis=0).reshape(nz * width)
    levels = convolve(padded, kernel, plane_rows) + bias[None, :]
    pooled = pool_pairs(levels).astype(jnp.bfloat16)

    coarse_rows = rows_here // 2
    pieces = pooled.reshape(nx, coarse_rows, nz * width)
    received = lax.all_to_all(pieces, "sx", 0, 0, tiled=False)
    received = jnp.roll(received.reshape(nx, coarse_rows, nz, width), me_z, axis=2)
    coarse = received.transpose(1, 2, 0, 3).reshape(coarse_rows, ch_out)

    attn_in = normalize(coarse.astype(jnp.float32), attn_gain).astype(jnp.bfloat16)
    proj = jnp.dot(sx_major(attn_in, nz, nx), proj_weight, preferred_element_type=jnp.float32)
    queries = proj[:, :q_cols].astype(jnp.bfloat16)
    keyvals = proj[:, q_cols:].astype(jnp.bfloat16)
    key_block = gather_rows(keyvals)
    key_block, out_z = lax.optimization_barrier((key_block, out_z))
    out_weight = lax.all_gather(out_z, "sx", axis=0, tiled=True)
    context = attend(queries, key_block, head_scale)
    projected = jnp.dot(sx_major(context, nz, nx), out_weight, preferred_element_type=jnp.float32)
    return (coarse, projected.astype(jnp.bfloat16))


def solution(mesh):
    dp = mesh.shape["dp"]
    seq = mesh.shape["seq"]
    nx = 8 if seq % 8 == 0 else seq
    nz = seq // nx
    grid = Mesh(mesh.devices.reshape(dp, nz, nx), ("dp", "sz", "sx"))
    rows = P(("dp", "sz", "sx"), None)
    return jax.shard_map(
        shards,
        mesh=grid,
        in_specs=(
            rows,
            P(),
            P(None, None, ("sz", "sx")),
            P(),
            P(),
            P(("sz", "sx"), None),
            P(("sz", "sx"), None),
            P(),
            P(("sz", "sx"), None),
        ),
        out_specs=(rows, rows),
        check_vma=False,
    )
```

```python
import jax
import jax.numpy as jnp
from jax import lax
from jax.sharding import Mesh
from jax.sharding import PartitionSpec as P

HEAD_DIM = 128


def normalize(values_in, channel_gain):
    meansq = jnp.mean(values_in * values_in, axis=-1, keepdims=True)
    return values_in * lax.rsqrt(meansq + 1e-06) * channel_gain


def convolve(padded, kernel, row_count):
    summed = jnp.zeros((row_count, kernel.shape[2]), jnp.float32)
    for kernel_tap in range(kernel.shape[0]):
        summed = summed + jnp.dot(
            padded[kernel_tap : kernel_tap + row_count],
            kernel[kernel_tap],
            preferred_element_type=jnp.float32,
        )
    return summed


def pool_pairs(levels):
    return jnp.max(levels.reshape(-1, 2, levels.shape[1]), axis=1)


def gather_rows(block):
    inner = lax.all_gather(block, "sx", axis=0, tiled=True)
    return lax.all_gather(inner, "sz", axis=0, tiled=True)


def sx_major(columns, nz, nx, me_z):
    rows = columns.shape[0]
    split = jnp.roll(columns.reshape(rows, nz, nx, -1), -me_z, axis=1)
    return split.transpose(0, 2, 1, 3).reshape(rows, columns.shape[1])


def attend(queries, key_block, scales):
    row_count = queries.shape[0]
    head_count = scales.shape[0]
    shaped = queries.reshape(row_count, head_count, HEAD_DIM)
    key_part = key_block[:, :HEAD_DIM]
    value_part = key_block[:, HEAD_DIM:]
    scores = (
        jnp.einsum("qhd,kd->hqk", shaped, key_part, preferred_element_type=jnp.float32)
        * scales[:, None, None]
        * HEAD_DIM ** (-0.5)
    )
    biggest = jnp.max(scores, axis=2)
    expon = jnp.exp(scores - biggest[:, :, None])
    total = jnp.sum(expon, axis=2)
    context = jnp.einsum(
        "hqk,kd->hqd", expon.astype(jnp.bfloat16), value_part, preferred_element_type=jnp.float32
    )
    context = context / total[:, :, None]
    return context.transpose(1, 0, 2).reshape(row_count, head_count * HEAD_DIM).astype(jnp.bfloat16)


def shards(
    features,
    norm_gain,
    conv_weight,
    conv_bias,
    attn_gain,
    query_weight,
    keyval_weight,
    head_scale,
    output_weight,
):
    nz = lax.axis_size("sz")
    nx = lax.axis_size("sx")
    me_x = lax.axis_index("sx")
    rows_here = features.shape[0]
    width = conv_weight.shape[2]
    ch_out = conv_bias.shape[0]

    me_z = lax.axis_index("sz")
    normed = jax.nn.gelu(normalize(features.astype(jnp.float32), norm_gain)).astype(jnp.bfloat16)
    plane = lax.all_gather(normed, "sx", axis=0, tiled=True)

    q_cols = query_weight.shape[1]
    lane = 256
    proj_piece = jnp.concatenate([query_weight, keyval_weight], axis=1)
    proj_n = proj_piece.size // lane
    both = jnp.concatenate(
        [proj_piece.reshape(proj_n, lane), output_weight.reshape(-1, lane)], axis=0
    )
    up = [(i, (i - 1) % nz) for i in range(nz)]
    down = [(i, (i + 1) % nz) for i in range(nz)]
    slots = {0: (conv_weight, both)}
    ahead = behind = slots[0]
    for step in range(1, nz // 2 + 1):
        ahead = lax.ppermute(ahead, "sz", up)
        slots[step % nz] = ahead
        if step <= (nz - 1) // 2:
            behind = lax.ppermute(behind, "sz", down)
            slots[(-step) % nz] = behind
    kernel = jnp.concatenate([slots[k][0] for k in range(nz)], axis=2)
    both_z = jnp.stack([slots[k][1] for k in range(nz)])
    proj_z = both_z[:, :proj_n].reshape(nz * proj_piece.shape[0], proj_piece.shape[1])
    out_z = both_z[:, proj_n:].reshape(nz * output_weight.shape[0], output_weight.shape[1])
    proj_weight = lax.all_gather(proj_z, "sx", axis=0, tiled=True)

    plane_rows = plane.shape[0]
    forward = [(i, i + 1) for i in range(nz - 1)]
    backward = [(i + 1, i) for i in range(nz - 1)]
    low = lax.ppermute(plane[plane_rows - 2 :], "sz", forward)
    high = lax.ppermute(plane[:2], "sz", backward)
    padded = jnp.concatenate([low, plane, high], axis=0)

    bias_all = conv_bias.reshape(nz, nx, width).transpose(1, 0, 2)
    bias = lax.dynamic_index_in_dim(bias_all, me_x, axis=0, keepdims=False)
    bias = jnp.roll(bias, -me_z, axis=0).reshape(nz * width)
    levels = convolve(padded, kernel, plane_rows) + bias[None, :]
    pooled = pool_pairs(levels).astype(jnp.bfloat16)

    coarse_rows = rows_here // 2
    pieces = pooled.reshape(nx, coarse_rows, nz * width)
    received = lax.all_to_all(pieces, "sx", 0, 0, tiled=False)
    received = jnp.roll(received.reshape(nx, coarse_rows, nz, width), me_z, axis=2)
    coarse = received.transpose(1, 2, 0, 3).reshape(coarse_rows, ch_out)

    attn_in = normalize(coarse.astype(jnp.float32), attn_gain).astype(jnp.bfloat16)
    proj = jnp.dot(sx_major(attn_in, nz, nx, me_z), proj_weight, preferred_element_type=jnp.float32)
    queries = proj[:, :q_cols].astype(jnp.bfloat16)
    keyvals = proj[:, q_cols:].astype(jnp.bfloat16)
    key_block = gather_rows(keyvals)
    key_block, out_z = lax.optimization_barrier((key_block, out_z))
    out_weight = lax.all_gather(out_z, "sx", axis=0, tiled=True)
    context = attend(queries, key_block, head_scale)
    projected = jnp.dot(sx_major(context, nz, nx, me_z), out_weight, preferred_element_type=jnp.float32)
    return (coarse, projected.astype(jnp.bfloat16))


def solution(mesh):
    dp = mesh.shape["dp"]
    seq = mesh.shape["seq"]
    nx = 8 if seq % 8 == 0 else seq
    nz = seq // nx
    grid = Mesh(mesh.devices.reshape(dp, nz, nx), ("dp", "sz", "sx"))
    rows = P(("dp", "sz", "sx"), None)
    return jax.shard_map(
        shards,
        mesh=grid,
        in_specs=(
            rows,
            P(),
            P(None, None, ("sz", "sx")),
            P(),
            P(),
            P(("sz", "sx"), None),
            P(("sz", "sx"), None),
            P(),
            P(("sz", "sx"), None),
        ),
        out_specs=(rows, rows),
        check_vma=False,
    )
```

```python
import jax
import jax.numpy as jnp
from jax import lax
from jax.experimental import pallas as pl
from jax.experimental.pallas import tpu as pltpu
from jax.sharding import Mesh
from jax.sharding import PartitionSpec as P

HEAD_DIM = 128


def normalize(values_in, channel_gain):
    meansq = jnp.mean(values_in * values_in, axis=-1, keepdims=True)
    return values_in * lax.rsqrt(meansq + 1e-06) * channel_gain


def convolve(padded, kernel, row_count):
    summed = jnp.zeros((row_count, kernel.shape[2]), jnp.float32)
    for kernel_tap in range(kernel.shape[0]):
        summed = summed + jnp.dot(
            padded[kernel_tap : kernel_tap + row_count],
            kernel[kernel_tap],
            preferred_element_type=jnp.float32,
        )
    return summed


def pool_pairs(levels):
    return jnp.max(levels.reshape(-1, 2, levels.shape[1]), axis=1)


def gather_rows(block):
    inner = lax.all_gather(block, "sx", axis=0, tiled=True)
    return lax.all_gather(inner, "sz", axis=0, tiled=True)


def sx_major(columns, nz, nx, me_z):
    rows = columns.shape[0]
    split = jnp.roll(columns.reshape(rows, nz, nx, -1), -me_z, axis=1)
    return split.transpose(0, 2, 1, 3).reshape(rows, columns.shape[1])


def head_kernel(scale_ref, q_ref, k_ref, v_ref, o_ref):
    head = pl.program_id(0)
    scores = lax.dot_general(
        q_ref[...], k_ref[...], (((1,), (1,)), ((), ())), preferred_element_type=jnp.float32
    )
    scores = scores * scale_ref[head] * HEAD_DIM ** (-0.5)
    biggest = jnp.max(scores, axis=1, keepdims=True)
    expon = jnp.exp(scores - biggest)
    total = jnp.sum(expon, axis=1, keepdims=True)
    context = jnp.dot(expon.astype(jnp.bfloat16), v_ref[...], preferred_element_type=jnp.float32)
    o_ref[...] = (context / total).astype(o_ref.dtype)


def attend(queries, key_block, scales):
    row_count = queries.shape[0]
    head_count = scales.shape[0]
    key_count = key_block.shape[0]
    flops = 4 * head_count * row_count * key_count * HEAD_DIM
    return pl.pallas_call(
        head_kernel,
        grid=(head_count,),
        in_specs=[
            pl.BlockSpec(memory_space=pltpu.SMEM),
            pl.BlockSpec((row_count, HEAD_DIM), lambda h: (0, h)),
            pl.BlockSpec((key_count, HEAD_DIM), lambda h: (0, 0)),
            pl.BlockSpec((key_count, HEAD_DIM), lambda h: (0, 1)),
        ],
        out_specs=pl.BlockSpec((row_count, HEAD_DIM), lambda h: (0, h)),
        out_shape=jax.ShapeDtypeStruct((row_count, head_count * HEAD_DIM), jnp.bfloat16),
        cost_estimate=pl.CostEstimate(
            flops=flops,
            transcendentals=head_count * row_count * key_count,
            bytes_accessed=2 * key_block.size + 4 * queries.size,
        ),
    )(scales, queries, key_block, key_block)


def shards(
    features,
    norm_gain,
    conv_weight,
    conv_bias,
    attn_gain,
    query_weight,
    keyval_weight,
    head_scale,
    output_weight,
):
    nz = lax.axis_size("sz")
    nx = lax.axis_size("sx")
    me_x = lax.axis_index("sx")
    rows_here = features.shape[0]
    width = conv_weight.shape[2]
    ch_out = conv_bias.shape[0]

    me_z = lax.axis_index("sz")
    normed = jax.nn.gelu(normalize(features.astype(jnp.float32), norm_gain)).astype(jnp.bfloat16)
    plane = lax.all_gather(normed, "sx", axis=0, tiled=True)

    q_cols = query_weight.shape[1]
    lane = 256
    proj_piece = jnp.concatenate([query_weight, keyval_weight], axis=1)
    proj_n = proj_piece.size // lane
    both = jnp.concatenate(
        [proj_piece.reshape(proj_n, lane), output_weight.reshape(-1, lane)], axis=0
    )
    up = [(i, (i - 1) % nz) for i in range(nz)]
    down = [(i, (i + 1) % nz) for i in range(nz)]
    slots = {0: (conv_weight, both)}
    ahead = behind = slots[0]
    for step in range(1, nz // 2 + 1):
        ahead = lax.ppermute(ahead, "sz", up)
        slots[step % nz] = ahead
        if step <= (nz - 1) // 2:
            behind = lax.ppermute(behind, "sz", down)
            slots[(-step) % nz] = behind
    kernel = jnp.concatenate([slots[k][0] for k in range(nz)], axis=2)
    both_z = jnp.stack([slots[k][1] for k in range(nz)])
    proj_z = both_z[:, :proj_n].reshape(nz * proj_piece.shape[0], proj_piece.shape[1])
    out_z = both_z[:, proj_n:].reshape(nz * output_weight.shape[0], output_weight.shape[1])
    proj_weight = lax.all_gather(proj_z, "sx", axis=0, tiled=True)

    plane_rows = plane.shape[0]
    forward = [(i, i + 1) for i in range(nz - 1)]
    backward = [(i + 1, i) for i in range(nz - 1)]
    low = lax.ppermute(plane[plane_rows - 2 :], "sz", forward)
    high = lax.ppermute(plane[:2], "sz", backward)
    padded = jnp.concatenate([low, plane, high], axis=0)

    bias_all = conv_bias.reshape(nz, nx, width).transpose(1, 0, 2)
    bias = lax.dynamic_index_in_dim(bias_all, me_x, axis=0, keepdims=False)
    bias = jnp.roll(bias, -me_z, axis=0).reshape(nz * width)
    levels = convolve(padded, kernel, plane_rows) + bias[None, :]
    pooled = pool_pairs(levels).astype(jnp.bfloat16)

    coarse_rows = rows_here // 2
    pieces = pooled.reshape(nx, coarse_rows, nz * width)
    received = lax.all_to_all(pieces, "sx", 0, 0, tiled=False)
    received = jnp.roll(received.reshape(nx, coarse_rows, nz, width), me_z, axis=2)
    coarse = received.transpose(1, 2, 0, 3).reshape(coarse_rows, ch_out)

    attn_in = normalize(coarse.astype(jnp.float32), attn_gain).astype(jnp.bfloat16)
    proj = jnp.dot(sx_major(attn_in, nz, nx, me_z), proj_weight, preferred_element_type=jnp.float32)
    queries = proj[:, :q_cols].astype(jnp.bfloat16)
    keyvals = proj[:, q_cols:].astype(jnp.bfloat16)
    key_block = gather_rows(keyvals)
    key_block, out_z = lax.optimization_barrier((key_block, out_z))
    out_weight = lax.all_gather(out_z, "sx", axis=0, tiled=True)
    context = attend(queries, key_block, head_scale)
    projected = jnp.dot(sx_major(context, nz, nx, me_z), out_weight, preferred_element_type=jnp.float32)
    return (coarse, projected.astype(jnp.bfloat16))


def solution(mesh):
    dp = mesh.shape["dp"]
    seq = mesh.shape["seq"]
    nx = 8 if seq % 8 == 0 else seq
    nz = seq // nx
    grid = Mesh(mesh.devices.reshape(dp, nz, nx), ("dp", "sz", "sx"))
    rows = P(("dp", "sz", "sx"), None)
    return jax.shard_map(
        shards,
        mesh=grid,
        in_specs=(
            rows,
            P(),
            P(None, None, ("sz", "sx")),
            P(),
            P(),
            P(("sz", "sx"), None),
            P(("sz", "sx"), None),
            P(),
            P(("sz", "sx"), None),
        ),
        out_specs=(rows, rows),
        check_vma=False,
    )
```

```python
import jax
import jax.numpy as jnp
from jax import lax
from jax.experimental import pallas as pl
from jax.experimental.pallas import tpu as pltpu
from jax.sharding import Mesh
from jax.sharding import PartitionSpec as P

HEAD_DIM = 128


def normalize(values_in, channel_gain):
    meansq = jnp.mean(values_in * values_in, axis=-1, keepdims=True)
    return values_in * lax.rsqrt(meansq + 1e-06) * channel_gain


def convolve(padded, kernel, row_count):
    summed = jnp.zeros((row_count, kernel.shape[2]), jnp.float32)
    for kernel_tap in range(kernel.shape[0]):
        summed = summed + jnp.dot(
            padded[kernel_tap : kernel_tap + row_count],
            kernel[kernel_tap],
            preferred_element_type=jnp.float32,
        )
    return summed


def pool_pairs(levels):
    return jnp.max(levels.reshape(-1, 2, levels.shape[1]), axis=1)


def gather_rows(block):
    inner = lax.all_gather(block, "sx", axis=0, tiled=True)
    return lax.all_gather(inner, "sz", axis=0, tiled=True)


def sx_major(columns, nz, nx, me_z):
    rows = columns.shape[0]
    split = jnp.roll(columns.reshape(rows, nz, nx, -1), -me_z, axis=1)
    return split.transpose(0, 2, 1, 3).reshape(rows, columns.shape[1])


def head_kernel(scale_ref, q_ref, k_ref, v_ref, o_ref):
    head = pl.program_id(0)
    scores = lax.dot_general(
        q_ref[...], k_ref[...], (((1,), (1,)), ((), ())), preferred_element_type=jnp.float32
    )
    scores = scores * scale_ref[head] * HEAD_DIM ** (-0.5)
    biggest = jnp.max(scores, axis=1, keepdims=True)
    expon = jnp.exp(scores - biggest)
    total = jnp.sum(expon, axis=1, keepdims=True)
    context = jnp.dot(expon.astype(jnp.bfloat16), v_ref[...], preferred_element_type=jnp.float32)
    o_ref[...] = (context / total).astype(o_ref.dtype)


def attend(queries, key_block, scales):
    row_count = queries.shape[0]
    head_count = scales.shape[0]
    key_count = key_block.shape[0]
    flops = 4 * head_count * row_count * key_count * HEAD_DIM
    return pl.pallas_call(
        head_kernel,
        grid=(head_count,),
        in_specs=[
            pl.BlockSpec(memory_space=pltpu.SMEM),
            pl.BlockSpec((row_count, HEAD_DIM), lambda h: (0, h)),
            pl.BlockSpec((key_count, HEAD_DIM), lambda h: (0, 0)),
            pl.BlockSpec((key_count, HEAD_DIM), lambda h: (0, 1)),
        ],
        out_specs=pl.BlockSpec((row_count, HEAD_DIM), lambda h: (0, h)),
        out_shape=jax.ShapeDtypeStruct((row_count, head_count * HEAD_DIM), jnp.bfloat16),
        cost_estimate=pl.CostEstimate(
            flops=flops,
            transcendentals=head_count * row_count * key_count,
            bytes_accessed=2 * key_block.size + 4 * queries.size,
        ),
    )(scales, queries, key_block, key_block)


def shards(
    features,
    norm_gain,
    conv_weight,
    conv_bias,
    attn_gain,
    query_weight,
    keyval_weight,
    head_scale,
    output_weight,
):
    nz = lax.axis_size("sz")
    nx = lax.axis_size("sx")
    me_x = lax.axis_index("sx")
    rows_here = features.shape[0]
    width = conv_weight.shape[2]
    ch_out = conv_bias.shape[0]

    me_z = lax.axis_index("sz")
    normed = jax.nn.gelu(normalize(features.astype(jnp.float32), norm_gain)).astype(jnp.bfloat16)
    plane = lax.all_gather(normed, "sx", axis=0, tiled=True)

    q_cols = query_weight.shape[1]
    lane = 256
    proj_piece = jnp.concatenate([query_weight, keyval_weight], axis=1)
    proj_n = proj_piece.size // lane
    both = jnp.concatenate(
        [proj_piece.reshape(proj_n, lane), output_weight.reshape(-1, lane)], axis=0
    )
    up = [(i, (i - 1) % nz) for i in range(nz)]
    down = [(i, (i + 1) % nz) for i in range(nz)]
    slots = {0: (conv_weight, both)}
    ahead = behind = slots[0]
    for step in range(1, nz // 2 + 1):
        ahead = lax.ppermute(ahead, "sz", up)
        if step <= (nz - 1) // 2:
            behind = lax.ppermute(behind, "sz", down)
            ahead, behind = lax.optimization_barrier((ahead, behind))
            slots[(-step) % nz] = behind
        else:
            ahead = lax.optimization_barrier(ahead)
        slots[step % nz] = ahead
    kernel = jnp.concatenate([slots[k][0] for k in range(nz)], axis=2)
    both_z = jnp.stack([slots[k][1] for k in range(nz)])
    proj_z = both_z[:, :proj_n].reshape(nz * proj_piece.shape[0], proj_piece.shape[1])
    out_z = both_z[:, proj_n:].reshape(nz * output_weight.shape[0], output_weight.shape[1])
    proj_weight = lax.all_gather(proj_z, "sx", axis=0, tiled=True)

    plane_rows = plane.shape[0]
    forward = [(i, i + 1) for i in range(nz - 1)]
    backward = [(i + 1, i) for i in range(nz - 1)]
    low = lax.ppermute(plane[plane_rows - 2 :], "sz", forward)
    high = lax.ppermute(plane[:2], "sz", backward)
    padded = jnp.concatenate([low, plane, high], axis=0)

    bias_all = conv_bias.reshape(nz, nx, width).transpose(1, 0, 2)
    bias = lax.dynamic_index_in_dim(bias_all, me_x, axis=0, keepdims=False)
    bias = jnp.roll(bias, -me_z, axis=0).reshape(nz * width)
    levels = convolve(padded, kernel, plane_rows) + bias[None, :]
    pooled = pool_pairs(levels).astype(jnp.bfloat16)
    pooled, out_z = lax.optimization_barrier((pooled, out_z))
    out_weight = lax.all_gather(out_z, "sx", axis=0, tiled=True)

    coarse_rows = rows_here // 2
    pieces = pooled.reshape(nx, coarse_rows, nz * width)
    received = lax.all_to_all(pieces, "sx", 0, 0, tiled=False)
    received = jnp.roll(received.reshape(nx, coarse_rows, nz, width), me_z, axis=2)
    coarse = received.transpose(1, 2, 0, 3).reshape(coarse_rows, ch_out)

    attn_in = normalize(coarse.astype(jnp.float32), attn_gain).astype(jnp.bfloat16)
    proj = jnp.dot(sx_major(attn_in, nz, nx, me_z), proj_weight, preferred_element_type=jnp.float32)
    queries = proj[:, :q_cols].astype(jnp.bfloat16)
    keyvals = proj[:, q_cols:].astype(jnp.bfloat16)
    keyvals, out_weight = lax.optimization_barrier((keyvals, out_weight))
    key_block = gather_rows(keyvals)
    context = attend(queries, key_block, head_scale)
    projected = jnp.dot(sx_major(context, nz, nx, me_z), out_weight, preferred_element_type=jnp.float32)
    return (coarse, projected.astype(jnp.bfloat16))


def solution(mesh):
    dp = mesh.shape["dp"]
    seq = mesh.shape["seq"]
    nx = 8 if seq % 8 == 0 else seq
    nz = seq // nx
    grid = Mesh(mesh.devices.reshape(dp, nz, nx), ("dp", "sz", "sx"))
    rows = P(("dp", "sz", "sx"), None)
    return jax.shard_map(
        shards,
        mesh=grid,
        in_specs=(
            rows,
            P(),
            P(None, None, ("sz", "sx")),
            P(),
            P(),
            P(("sz", "sx"), None),
            P(("sz", "sx"), None),
            P(),
            P(("sz", "sx"), None),
        ),
        out_specs=(rows, rows),
        check_vma=False,
    )
```

```python
import jax
import jax.numpy as jnp
from jax import lax
from jax.experimental import pallas as pl
from jax.experimental.pallas import tpu as pltpu
from jax.sharding import Mesh
from jax.sharding import PartitionSpec as P

HEAD_DIM = 128


def normalize(values_in, channel_gain):
    meansq = jnp.mean(values_in * values_in, axis=-1, keepdims=True)
    return values_in * lax.rsqrt(meansq + 1e-06) * channel_gain


def convolve(padded, kernel, row_count):
    summed = jnp.zeros((row_count, kernel.shape[2]), jnp.float32)
    for kernel_tap in range(kernel.shape[0]):
        summed = summed + jnp.dot(
            padded[kernel_tap : kernel_tap + row_count],
            kernel[kernel_tap],
            preferred_element_type=jnp.float32,
        )
    return summed


def pool_pairs(levels):
    return jnp.max(levels.reshape(-1, 2, levels.shape[1]), axis=1)


def gather_rows(block):
    inner = lax.all_gather(block, "sx", axis=0, tiled=True)
    return lax.all_gather(inner, "sz", axis=0, tiled=True)


def sx_major(columns, nz, nx, me_z):
    rows = columns.shape[0]
    split = jnp.roll(columns.reshape(rows, nz, nx, -1), -me_z, axis=1)
    return split.transpose(0, 2, 1, 3).reshape(rows, columns.shape[1])


def ring(value, axis, n):
    up = [(i, (i - 1) % n) for i in range(n)]
    down = [(i, (i + 1) % n) for i in range(n)]
    slots = {0: value}
    ahead = behind = value
    for step in range(1, n // 2 + 1):
        ahead = lax.ppermute(ahead, axis, up)
        if step <= (n - 1) // 2:
            behind = lax.ppermute(behind, axis, down)
            ahead, behind = lax.optimization_barrier((ahead, behind))
            slots[(-step) % n] = behind
        else:
            ahead = lax.optimization_barrier(ahead)
        slots[step % n] = ahead
    return [slots[k] for k in range(n)]


def head_kernel(scale_ref, q_ref, k_ref, v_ref, o_ref):
    head = pl.program_id(0)
    scores = lax.dot_general(
        q_ref[...], k_ref[...], (((1,), (1,)), ((), ())), preferred_element_type=jnp.float32
    )
    scores = scores * scale_ref[head] * HEAD_DIM ** (-0.5)
    biggest = jnp.max(scores, axis=1, keepdims=True)
    expon = jnp.exp(scores - biggest)
    total = jnp.sum(expon, axis=1, keepdims=True)
    context = jnp.dot(expon.astype(jnp.bfloat16), v_ref[...], preferred_element_type=jnp.float32)
    o_ref[...] = (context / total).astype(o_ref.dtype)


def attend(queries, key_block, scales):
    row_count = queries.shape[0]
    head_count = scales.shape[0]
    key_count = key_block.shape[0]
    flops = 4 * head_count * row_count * key_count * HEAD_DIM
    return pl.pallas_call(
        head_kernel,
        grid=(head_count,),
        in_specs=[
            pl.BlockSpec(memory_space=pltpu.SMEM),
            pl.BlockSpec((row_count, HEAD_DIM), lambda h: (0, h)),
            pl.BlockSpec((key_count, HEAD_DIM), lambda h: (0, 0)),
            pl.BlockSpec((key_count, HEAD_DIM), lambda h: (0, 1)),
        ],
        out_specs=pl.BlockSpec((row_count, HEAD_DIM), lambda h: (0, h)),
        out_shape=jax.ShapeDtypeStruct((row_count, head_count * HEAD_DIM), jnp.bfloat16),
        cost_estimate=pl.CostEstimate(
            flops=flops,
            transcendentals=head_count * row_count * key_count,
            bytes_accessed=2 * key_block.size + 4 * queries.size,
        ),
    )(scales, queries, key_block, key_block)


def shards(
    features,
    norm_gain,
    conv_weight,
    conv_bias,
    attn_gain,
    query_weight,
    keyval_weight,
    head_scale,
    output_weight,
):
    nz = lax.axis_size("sz")
    nx = lax.axis_size("sx")
    me_x = lax.axis_index("sx")
    rows_here = features.shape[0]
    width = conv_weight.shape[2]
    ch_out = conv_bias.shape[0]

    me_z = lax.axis_index("sz")
    normed = jax.nn.gelu(normalize(features.astype(jnp.float32), norm_gain)).astype(jnp.bfloat16)
    plane = lax.all_gather(normed, "sx", axis=0, tiled=True)

    q_cols = query_weight.shape[1]
    lane = 256
    proj_piece = jnp.concatenate([query_weight, keyval_weight], axis=1)
    proj_n = proj_piece.size // lane
    both = jnp.concatenate(
        [proj_piece.reshape(proj_n, lane), output_weight.reshape(-1, lane)], axis=0
    )
    slots = ring((conv_weight, both), "sz", nz)
    kernel = jnp.concatenate([s[0] for s in slots], axis=2)
    both_z = jnp.stack([s[1] for s in slots])
    proj_z = both_z[:, :proj_n].reshape(nz * proj_piece.shape[0], proj_piece.shape[1])
    out_z = both_z[:, proj_n:].reshape(nz * output_weight.shape[0], output_weight.shape[1])
    proj_weight = lax.all_gather(proj_z, "sx", axis=0, tiled=True)

    plane_rows = plane.shape[0]
    forward = [(i, i + 1) for i in range(nz - 1)]
    backward = [(i + 1, i) for i in range(nz - 1)]
    low = lax.ppermute(plane[plane_rows - 2 :], "sz", forward)
    high = lax.ppermute(plane[:2], "sz", backward)
    padded = jnp.concatenate([low, plane, high], axis=0)

    bias_all = conv_bias.reshape(nz, nx, width).transpose(1, 0, 2)
    bias = lax.dynamic_index_in_dim(bias_all, me_x, axis=0, keepdims=False)
    bias = jnp.roll(bias, -me_z, axis=0).reshape(nz * width)
    levels = convolve(padded, kernel, plane_rows) + bias[None, :]
    pooled = pool_pairs(levels).astype(jnp.bfloat16)

    coarse_rows = rows_here // 2
    pieces = pooled.reshape(nx, coarse_rows, nz * width)
    received = lax.all_to_all(pieces, "sx", 0, 0, tiled=False)
    received = jnp.roll(received.reshape(nx, coarse_rows, nz, width), me_z, axis=2)
    coarse = received.transpose(1, 2, 0, 3).reshape(coarse_rows, ch_out)

    attn_in = normalize(coarse.astype(jnp.float32), attn_gain).astype(jnp.bfloat16)
    proj = jnp.dot(sx_major(attn_in, nz, nx, me_z), proj_weight, preferred_element_type=jnp.float32)
    queries = proj[:, :q_cols].astype(jnp.bfloat16)
    keyvals = proj[:, q_cols:].astype(jnp.bfloat16)
    kv_plane = lax.all_gather(keyvals, "sx", axis=0, tiled=True)
    kv_plane, out_z = lax.optimization_barrier((kv_plane, out_z))
    key_block = lax.all_gather(kv_plane, "sz", axis=0, tiled=True)
    out_weight = jnp.concatenate(ring(out_z, "sx", nx), axis=0)
    context = attend(queries, key_block, head_scale)
    rows = context.shape[0]
    by_slot = jnp.roll(context.reshape(rows, nz, nx, -1), (-me_z, -me_x), axis=(1, 2))
    by_slot = by_slot.transpose(0, 2, 1, 3).reshape(rows, context.shape[1])
    projected = jnp.dot(by_slot, out_weight, preferred_element_type=jnp.float32)
    return (coarse, projected.astype(jnp.bfloat16))


def solution(mesh):
    dp = mesh.shape["dp"]
    seq = mesh.shape["seq"]
    nx = 8 if seq % 8 == 0 else seq
    nz = seq // nx
    grid = Mesh(mesh.devices.reshape(dp, nz, nx), ("dp", "sz", "sx"))
    rows = P(("dp", "sz", "sx"), None)
    return jax.shard_map(
        shards,
        mesh=grid,
        in_specs=(
            rows,
            P(),
            P(None, None, ("sz", "sx")),
            P(),
            P(),
            P(("sz", "sx"), None),
            P(("sz", "sx"), None),
            P(),
            P(("sz", "sx"), None),
        ),
        out_specs=(rows, rows),
        check_vma=False,
    )
```

```python
import jax
import jax.numpy as jnp
from jax import lax
from jax.experimental import pallas as pl
from jax.experimental.pallas import tpu as pltpu
from jax.sharding import Mesh
from jax.sharding import PartitionSpec as P

HEAD_DIM = 128


def normalize(values_in, channel_gain):
    meansq = jnp.mean(values_in * values_in, axis=-1, keepdims=True)
    return values_in * lax.rsqrt(meansq + 1e-06) * channel_gain


def convolve(padded, kernel, row_count):
    summed = jnp.zeros((row_count, kernel.shape[2]), jnp.float32)
    for kernel_tap in range(kernel.shape[0]):
        summed = summed + jnp.dot(
            padded[kernel_tap : kernel_tap + row_count],
            kernel[kernel_tap],
            preferred_element_type=jnp.float32,
        )
    return summed


def pool_pairs(levels):
    return jnp.max(levels.reshape(-1, 2, levels.shape[1]), axis=1)


def gather_rows(block):
    inner = lax.all_gather(block, "sx", axis=0, tiled=True)
    return lax.all_gather(inner, "sz", axis=0, tiled=True)


def sx_major(columns, nz, nx, me_z):
    rows = columns.shape[0]
    split = jnp.roll(columns.reshape(rows, nz, nx, -1), -me_z, axis=1)
    return split.transpose(0, 2, 1, 3).reshape(rows, columns.shape[1])


def ring(value, axis, n):
    up = [(i, (i - 1) % n) for i in range(n)]
    down = [(i, (i + 1) % n) for i in range(n)]
    slots = {0: value}
    ahead = behind = value
    for step in range(1, n // 2 + 1):
        ahead = lax.ppermute(ahead, axis, up)
        if step <= (n - 1) // 2:
            behind = lax.ppermute(behind, axis, down)
            ahead, behind = lax.optimization_barrier((ahead, behind))
            slots[(-step) % n] = behind
        else:
            ahead = lax.optimization_barrier(ahead)
        slots[step % n] = ahead
    return [slots[k] for k in range(n)]


def head_kernel(scale_ref, q_ref, k_ref, v_ref, o_ref):
    head = pl.program_id(0)
    scores = lax.dot_general(
        q_ref[...], k_ref[...], (((1,), (1,)), ((), ())), preferred_element_type=jnp.float32
    )
    scores = scores * scale_ref[head] * HEAD_DIM ** (-0.5)
    biggest = jnp.max(scores, axis=1, keepdims=True)
    expon = jnp.exp(scores - biggest)
    total = jnp.sum(expon, axis=1, keepdims=True)
    context = jnp.dot(expon.astype(jnp.bfloat16), v_ref[...], preferred_element_type=jnp.float32)
    o_ref[...] = (context / total).astype(o_ref.dtype)


def attend(queries, keys_all, values_all, scales):
    row_count = queries.shape[0]
    head_count = scales.shape[0]
    key_count = keys_all.shape[0]
    flops = 4 * head_count * row_count * key_count * HEAD_DIM
    return pl.pallas_call(
        head_kernel,
        grid=(head_count,),
        in_specs=[
            pl.BlockSpec(memory_space=pltpu.SMEM),
            pl.BlockSpec((row_count, HEAD_DIM), lambda h: (0, h)),
            pl.BlockSpec((key_count, HEAD_DIM), lambda h: (0, 0)),
            pl.BlockSpec((key_count, HEAD_DIM), lambda h: (0, 0)),
        ],
        out_specs=pl.BlockSpec((row_count, HEAD_DIM), lambda h: (0, h)),
        out_shape=jax.ShapeDtypeStruct((row_count, head_count * HEAD_DIM), jnp.bfloat16),
        cost_estimate=pl.CostEstimate(
            flops=flops,
            transcendentals=head_count * row_count * key_count,
            bytes_accessed=2 * (keys_all.size + values_all.size) + 4 * queries.size,
        ),
    )(scales, queries, keys_all, values_all)


def shards(
    features,
    norm_gain,
    conv_weight,
    conv_bias,
    attn_gain,
    query_weight,
    keyval_weight,
    head_scale,
    output_weight,
):
    nz = lax.axis_size("sz")
    nx = lax.axis_size("sx")
    me_x = lax.axis_index("sx")
    rows_here = features.shape[0]
    width = conv_weight.shape[2]
    ch_out = conv_bias.shape[0]

    me_z = lax.axis_index("sz")
    normed = jax.nn.gelu(normalize(features.astype(jnp.float32), norm_gain)).astype(jnp.bfloat16)
    plane = lax.all_gather(normed, "sx", axis=0, tiled=True)

    q_cols = query_weight.shape[1]
    lane = 256
    proj_piece = jnp.concatenate([query_weight, keyval_weight], axis=1)
    proj_n = proj_piece.size // lane
    both = jnp.concatenate(
        [proj_piece.reshape(proj_n, lane), output_weight.reshape(-1, lane)], axis=0
    )
    slots = ring((conv_weight, both), "sz", nz)
    kernel = jnp.concatenate([s[0] for s in slots], axis=2)
    both_z = jnp.stack([s[1] for s in slots])
    proj_z = both_z[:, :proj_n].reshape(nz * proj_piece.shape[0], proj_piece.shape[1])
    out_z = both_z[:, proj_n:].reshape(nz * output_weight.shape[0], output_weight.shape[1])
    proj_weight = lax.all_gather(proj_z, "sx", axis=0, tiled=True)

    plane_rows = plane.shape[0]
    forward = [(i, i + 1) for i in range(nz - 1)]
    backward = [(i + 1, i) for i in range(nz - 1)]
    low = lax.ppermute(plane[plane_rows - 2 :], "sz", forward)
    high = lax.ppermute(plane[:2], "sz", backward)
    padded = jnp.concatenate([low, plane, high], axis=0)

    bias_all = conv_bias.reshape(nz, nx, width).transpose(1, 0, 2)
    bias = lax.dynamic_index_in_dim(bias_all, me_x, axis=0, keepdims=False)
    bias = jnp.roll(bias, -me_z, axis=0).reshape(nz * width)
    levels = convolve(padded, kernel, plane_rows) + bias[None, :]
    pooled = pool_pairs(levels).astype(jnp.bfloat16)

    coarse_rows = rows_here // 2
    pieces = pooled.reshape(nx, coarse_rows, nz * width)
    received = lax.all_to_all(pieces, "sx", 0, 0, tiled=False)
    received = jnp.roll(received.reshape(nx, coarse_rows, nz, width), me_z, axis=2)
    coarse = received.transpose(1, 2, 0, 3).reshape(coarse_rows, ch_out)

    attn_in = normalize(coarse.astype(jnp.float32), attn_gain).astype(jnp.bfloat16)
    proj = jnp.dot(sx_major(attn_in, nz, nx, me_z), proj_weight, preferred_element_type=jnp.float32)
    queries = proj[:, :q_cols].astype(jnp.bfloat16)
    keyvals = proj[:, q_cols:].astype(jnp.bfloat16)
    kv_plane = lax.all_gather(keyvals, "sx", axis=0, tiled=True)
    kv_plane, out_z = lax.optimization_barrier((kv_plane, out_z))
    keys_all = lax.all_gather(kv_plane[:, :HEAD_DIM], "sz", axis=0, tiled=True)
    value_slots = jnp.stack(ring(kv_plane[:, HEAD_DIM:], "sz", nz))
    values_all = jnp.roll(value_slots, me_z, axis=0).reshape(keys_all.shape)
    out_weight = jnp.concatenate(ring(out_z, "sx", nx), axis=0)
    context = attend(queries, keys_all, values_all, head_scale)
    rows = context.shape[0]
    by_slot = jnp.roll(context.reshape(rows, nz, nx, -1), (-me_z, -me_x), axis=(1, 2))
    by_slot = by_slot.transpose(0, 2, 1, 3).reshape(rows, context.shape[1])
    projected = jnp.dot(by_slot, out_weight, preferred_element_type=jnp.float32)
    return (coarse, projected.astype(jnp.bfloat16))


def solution(mesh):
    dp = mesh.shape["dp"]
    seq = mesh.shape["seq"]
    nx = 8 if seq % 8 == 0 else seq
    nz = seq // nx
    grid = Mesh(mesh.devices.reshape(dp, nz, nx), ("dp", "sz", "sx"))
    rows = P(("dp", "sz", "sx"), None)
    return jax.shard_map(
        shards,
        mesh=grid,
        in_specs=(
            rows,
            P(),
            P(None, None, ("sz", "sx")),
            P(),
            P(),
            P(("sz", "sx"), None),
            P(("sz", "sx"), None),
            P(),
            P(("sz", "sx"), None),
        ),
        out_specs=(rows, rows),
        check_vma=False,
    )
```

```python
import jax
import jax.numpy as jnp
from jax import lax
from jax.experimental import pallas as pl
from jax.experimental.pallas import tpu as pltpu
from jax.sharding import Mesh
from jax.sharding import PartitionSpec as P

HEAD_DIM = 128


def normalize(values_in, channel_gain):
    meansq = jnp.mean(values_in * values_in, axis=-1, keepdims=True)
    return values_in * lax.rsqrt(meansq + 1e-06) * channel_gain


def convolve(padded, kernel, row_count):
    summed = jnp.zeros((row_count, kernel.shape[2]), jnp.float32)
    for kernel_tap in range(kernel.shape[0]):
        summed = summed + jnp.dot(
            padded[kernel_tap : kernel_tap + row_count],
            kernel[kernel_tap],
            preferred_element_type=jnp.float32,
        )
    return summed


def pool_pairs(levels):
    return jnp.max(levels.reshape(-1, 2, levels.shape[1]), axis=1)


def gather_rows(block):
    inner = lax.all_gather(block, "sx", axis=0, tiled=True)
    return lax.all_gather(inner, "sz", axis=0, tiled=True)


def sx_major(columns, nz, nx, me_z):
    rows = columns.shape[0]
    split = jnp.roll(columns.reshape(rows, nz, nx, -1), -me_z, axis=1)
    return split.transpose(0, 2, 1, 3).reshape(rows, columns.shape[1])


def split_at(a):
    half = a.shape[0] // 2
    return half if a.shape[0] < 32 else half // 16 * 16


def ring(value, axis, n):
    up = [(i, (i - 1) % n) for i in range(n)]
    down = [(i, (i + 1) % n) for i in range(n)]
    slots = {0: value}
    ahead = behind = value
    for step in range(1, n // 2 + 1):
        if step > (n - 1) // 2 and n > 2:
            ahead = ahead
        else:
            ahead = lax.ppermute(ahead, axis, up)
        if step <= (n - 1) // 2:
            behind = lax.ppermute(behind, axis, down)
            ahead, behind = lax.optimization_barrier((ahead, behind))
            slots[(-step) % n] = behind
        elif n == 2:
            ahead = lax.optimization_barrier(ahead)
        else:
            first = jax.tree.map(lambda a: a[: split_at(a)], ahead)
            second = jax.tree.map(lambda a: a[split_at(a) :], behind)
            first = lax.ppermute(first, axis, up)
            second = lax.ppermute(second, axis, down)
            first, second = lax.optimization_barrier((first, second))
            ahead = jax.tree.map(lambda a, b: jnp.concatenate([a, b], axis=0), first, second)
            slots[step % n] = ahead
            continue
        slots[step % n] = ahead
    return [slots[k] for k in range(n)]


def head_kernel(scale_ref, q_ref, k_ref, v_ref, o_ref):
    head = pl.program_id(0)
    scores = lax.dot_general(
        q_ref[...], k_ref[...], (((1,), (1,)), ((), ())), preferred_element_type=jnp.float32
    )
    scores = scores * scale_ref[head] * HEAD_DIM ** (-0.5)
    biggest = jnp.max(scores, axis=1, keepdims=True)
    expon = jnp.exp(scores - biggest)
    total = jnp.sum(expon, axis=1, keepdims=True)
    context = jnp.dot(expon.astype(jnp.bfloat16), v_ref[...], preferred_element_type=jnp.float32)
    o_ref[...] = (context / total).astype(o_ref.dtype)


def attend(queries, key_block, scales):
    row_count = queries.shape[0]
    head_count = scales.shape[0]
    key_count = key_block.shape[0]
    flops = 4 * head_count * row_count * key_count * HEAD_DIM
    return pl.pallas_call(
        head_kernel,
        grid=(head_count,),
        in_specs=[
            pl.BlockSpec(memory_space=pltpu.SMEM),
            pl.BlockSpec((row_count, HEAD_DIM), lambda h: (0, h)),
            pl.BlockSpec((key_count, HEAD_DIM), lambda h: (0, 0)),
            pl.BlockSpec((key_count, HEAD_DIM), lambda h: (0, 1)),
        ],
        out_specs=pl.BlockSpec((row_count, HEAD_DIM), lambda h: (0, h)),
        out_shape=jax.ShapeDtypeStruct((row_count, head_count * HEAD_DIM), jnp.bfloat16),
        cost_estimate=pl.CostEstimate(
            flops=flops,
            transcendentals=head_count * row_count * key_count,
            bytes_accessed=2 * key_block.size + 4 * queries.size,
        ),
    )(scales, queries, key_block, key_block)


def shards(
    features,
    norm_gain,
    conv_weight,
    conv_bias,
    attn_gain,
    query_weight,
    keyval_weight,
    head_scale,
    output_weight,
):
    nz = lax.axis_size("sz")
    nx = lax.axis_size("sx")
    me_x = lax.axis_index("sx")
    rows_here = features.shape[0]
    width = conv_weight.shape[2]
    ch_out = conv_bias.shape[0]

    me_z = lax.axis_index("sz")
    normed = jax.nn.gelu(normalize(features.astype(jnp.float32), norm_gain)).astype(jnp.bfloat16)
    plane = lax.all_gather(normed, "sx", axis=0, tiled=True)

    q_cols = query_weight.shape[1]
    lane = 256
    proj_piece = jnp.concatenate([query_weight, keyval_weight], axis=1)
    proj_n = proj_piece.size // lane
    both = jnp.concatenate(
        [proj_piece.reshape(proj_n, lane), output_weight.reshape(-1, lane)], axis=0
    )
    slots = ring((conv_weight, both), "sz", nz)
    kernel = jnp.concatenate([s[0] for s in slots], axis=2)
    both_z = jnp.stack([s[1] for s in slots])
    proj_z = both_z[:, :proj_n].reshape(nz * proj_piece.shape[0], proj_piece.shape[1])
    out_z = both_z[:, proj_n:].reshape(nz * output_weight.shape[0], output_weight.shape[1])
    proj_weight = lax.all_gather(proj_z, "sx", axis=0, tiled=True)

    plane_rows = plane.shape[0]
    forward = [(i, i + 1) for i in range(nz - 1)]
    backward = [(i + 1, i) for i in range(nz - 1)]
    low = lax.ppermute(plane[plane_rows - 2 :], "sz", forward)
    high = lax.ppermute(plane[:2], "sz", backward)
    padded = jnp.concatenate([low, plane, high], axis=0)

    bias_all = conv_bias.reshape(nz, nx, width).transpose(1, 0, 2)
    bias = lax.dynamic_index_in_dim(bias_all, me_x, axis=0, keepdims=False)
    bias = jnp.roll(bias, -me_z, axis=0).reshape(nz * width)
    levels = convolve(padded, kernel, plane_rows) + bias[None, :]
    pooled = pool_pairs(levels).astype(jnp.bfloat16)

    coarse_rows = rows_here // 2
    pieces = pooled.reshape(nx, coarse_rows, nz * width)
    received = lax.all_to_all(pieces, "sx", 0, 0, tiled=False)
    received = jnp.roll(received.reshape(nx, coarse_rows, nz, width), me_z, axis=2)
    coarse = received.transpose(1, 2, 0, 3).reshape(coarse_rows, ch_out)

    attn_in = normalize(coarse.astype(jnp.float32), attn_gain).astype(jnp.bfloat16)
    proj = jnp.dot(sx_major(attn_in, nz, nx, me_z), proj_weight, preferred_element_type=jnp.float32)
    queries = proj[:, :q_cols].astype(jnp.bfloat16)
    keyvals = proj[:, q_cols:].astype(jnp.bfloat16)
    kv_plane = lax.all_gather(keyvals, "sx", axis=0, tiled=True)
    kv_plane, out_z = lax.optimization_barrier((kv_plane, out_z))
    key_block = lax.all_gather(kv_plane, "sz", axis=0, tiled=True)
    out_weight = jnp.concatenate(ring(out_z, "sx", nx), axis=0)
    context = attend(queries, key_block, head_scale)
    rows = context.shape[0]
    by_slot = jnp.roll(context.reshape(rows, nz, nx, -1), (-me_z, -me_x), axis=(1, 2))
    by_slot = by_slot.transpose(0, 2, 1, 3).reshape(rows, context.shape[1])
    projected = jnp.dot(by_slot, out_weight, preferred_element_type=jnp.float32)
    return (coarse, projected.astype(jnp.bfloat16))


def solution(mesh):
    dp = mesh.shape["dp"]
    seq = mesh.shape["seq"]
    nx = 8 if seq % 8 == 0 else seq
    nz = seq // nx
    grid = Mesh(mesh.devices.reshape(dp, nz, nx), ("dp", "sz", "sx"))
    rows = P(("dp", "sz", "sx"), None)
    return jax.shard_map(
        shards,
        mesh=grid,
        in_specs=(
            rows,
            P(),
            P(None, None, ("sz", "sx")),
            P(),
            P(),
            P(("sz", "sx"), None),
            P(("sz", "sx"), None),
            P(),
            P(("sz", "sx"), None),
        ),
        out_specs=(rows, rows),
        check_vma=False,
    )
```

```python
import jax
import jax.numpy as jnp
from jax import lax
from jax.experimental import pallas as pl
from jax.experimental.pallas import tpu as pltpu
from jax.sharding import Mesh
from jax.sharding import PartitionSpec as P

HEAD_DIM = 128


def normalize(values_in, channel_gain):
    meansq = jnp.mean(values_in * values_in, axis=-1, keepdims=True)
    return values_in * lax.rsqrt(meansq + 1e-06) * channel_gain


def convolve(padded, kernel, row_count):
    summed = jnp.zeros((row_count, kernel.shape[2]), jnp.float32)
    for kernel_tap in range(kernel.shape[0]):
        summed = summed + jnp.dot(
            padded[kernel_tap : kernel_tap + row_count],
            kernel[kernel_tap],
            preferred_element_type=jnp.float32,
        )
    return summed


def pool_pairs(levels):
    return jnp.max(levels.reshape(-1, 2, levels.shape[1]), axis=1)


def gather_rows(block):
    inner = lax.all_gather(block, "sx", axis=0, tiled=True)
    return lax.all_gather(inner, "sz", axis=0, tiled=True)


def sx_major(columns, nz, nx, me_z):
    rows = columns.shape[0]
    split = jnp.roll(columns.reshape(rows, nz, nx, -1), -me_z, axis=1)
    return split.transpose(0, 2, 1, 3).reshape(rows, columns.shape[1])


def ring(value, axis, n):
    up = [(i, (i - 1) % n) for i in range(n)]
    down = [(i, (i + 1) % n) for i in range(n)]
    slots = {0: value}
    ahead = behind = value
    for step in range(1, n // 2 + 1):
        ahead = lax.ppermute(ahead, axis, up)
        if step <= (n - 1) // 2:
            behind = lax.ppermute(behind, axis, down)
            ahead, behind = lax.optimization_barrier((ahead, behind))
            slots[(-step) % n] = behind
        else:
            ahead = lax.optimization_barrier(ahead)
        slots[step % n] = ahead
    return [slots[k] for k in range(n)]


def head_kernel(scale_ref, q_ref, k_ref, v_ref, o_ref):
    head = pl.program_id(0)
    scores = lax.dot_general(
        q_ref[...], k_ref[...], (((1,), (1,)), ((), ())), preferred_element_type=jnp.float32
    )
    scores = scores * scale_ref[head] * HEAD_DIM ** (-0.5)
    biggest = jnp.max(scores, axis=1, keepdims=True)
    expon = jnp.exp(scores - biggest)
    total = jnp.sum(expon, axis=1, keepdims=True)
    context = jnp.dot(expon.astype(jnp.bfloat16), v_ref[...], preferred_element_type=jnp.float32)
    o_ref[...] = (context / total).astype(o_ref.dtype)


def attend(queries, key_block, scales):
    row_count = queries.shape[0]
    head_count = scales.shape[0]
    key_count = key_block.shape[0]
    flops = 4 * head_count * row_count * key_count * HEAD_DIM
    return pl.pallas_call(
        head_kernel,
        grid=(head_count,),
        in_specs=[
            pl.BlockSpec(memory_space=pltpu.SMEM),
            pl.BlockSpec((row_count, HEAD_DIM), lambda h: (0, h)),
            pl.BlockSpec((key_count, HEAD_DIM), lambda h: (0, 0)),
            pl.BlockSpec((key_count, HEAD_DIM), lambda h: (0, 1)),
        ],
        out_specs=pl.BlockSpec((row_count, HEAD_DIM), lambda h: (0, h)),
        out_shape=jax.ShapeDtypeStruct((row_count, head_count * HEAD_DIM), jnp.bfloat16),
        cost_estimate=pl.CostEstimate(
            flops=flops,
            transcendentals=head_count * row_count * key_count,
            bytes_accessed=2 * key_block.size + 4 * queries.size,
        ),
    )(scales, queries, key_block, key_block)


def shards(
    features,
    norm_gain,
    conv_weight,
    conv_bias,
    attn_gain,
    query_weight,
    keyval_weight,
    head_scale,
    output_weight,
):
    nz = lax.axis_size("sz")
    nx = lax.axis_size("sx")
    me_x = lax.axis_index("sx")
    rows_here = features.shape[0]
    width = conv_weight.shape[2]
    ch_out = conv_bias.shape[0]

    me_z = lax.axis_index("sz")
    normed = jax.nn.gelu(normalize(features.astype(jnp.float32), norm_gain)).astype(jnp.bfloat16)
    count = nz * nx
    after = [(i, i + 1) for i in range(count - 1)]
    before = [(i + 1, i) for i in range(count - 1)]
    low = lax.ppermute(normed[rows_here - 2 :], ("sz", "sx"), after)
    high = lax.ppermute(normed[:2], ("sz", "sx"), before)
    framed = lax.all_gather(jnp.concatenate([low, normed, high], axis=0), "sx", axis=0, tiled=False)

    q_cols = query_weight.shape[1]
    lane = 256
    proj_piece = jnp.concatenate([query_weight, keyval_weight], axis=1)
    proj_n = proj_piece.size // lane
    both = jnp.concatenate(
        [proj_piece.reshape(proj_n, lane), output_weight.reshape(-1, lane)], axis=0
    )
    slots = ring((conv_weight, both), "sz", nz)
    kernel = jnp.concatenate([s[0] for s in slots], axis=2)
    both_z = jnp.stack([s[1] for s in slots])
    proj_z = both_z[:, :proj_n].reshape(nz * proj_piece.shape[0], proj_piece.shape[1])
    out_z = both_z[:, proj_n:].reshape(nz * output_weight.shape[0], output_weight.shape[1])
    proj_weight = lax.all_gather(proj_z, "sx", axis=0, tiled=True)

    plane_rows = nx * rows_here
    padded = jnp.concatenate(
        [framed[0, :2], framed[:, 2 : rows_here + 2].reshape(plane_rows, -1), framed[nx - 1, rows_here + 2 :]],
        axis=0,
    )

    bias_all = conv_bias.reshape(nz, nx, width).transpose(1, 0, 2)
    bias = lax.dynamic_index_in_dim(bias_all, me_x, axis=0, keepdims=False)
    bias = jnp.roll(bias, -me_z, axis=0).reshape(nz * width)
    levels = convolve(padded, kernel, plane_rows) + bias[None, :]
    pooled = pool_pairs(levels).astype(jnp.bfloat16)

    coarse_rows = rows_here // 2
    pieces = pooled.reshape(nx, coarse_rows, nz * width)
    received = lax.all_to_all(pieces, "sx", 0, 0, tiled=False)
    received = jnp.roll(received.reshape(nx, coarse_rows, nz, width), me_z, axis=2)
    coarse = received.transpose(1, 2, 0, 3).reshape(coarse_rows, ch_out)

    attn_in = normalize(coarse.astype(jnp.float32), attn_gain).astype(jnp.bfloat16)
    proj = jnp.dot(sx_major(attn_in, nz, nx, me_z), proj_weight, preferred_element_type=jnp.float32)
    queries = proj[:, :q_cols].astype(jnp.bfloat16)
    keyvals = proj[:, q_cols:].astype(jnp.bfloat16)
    kv_plane = lax.all_gather(keyvals, "sx", axis=0, tiled=True)
    kv_plane, out_z = lax.optimization_barrier((kv_plane, out_z))
    key_block = lax.all_gather(kv_plane, "sz", axis=0, tiled=True)
    out_weight = jnp.concatenate(ring(out_z, "sx", nx), axis=0)
    context = attend(queries, key_block, head_scale)
    rows = context.shape[0]
    by_slot = jnp.roll(context.reshape(rows, nz, nx, -1), (-me_z, -me_x), axis=(1, 2))
    by_slot = by_slot.transpose(0, 2, 1, 3).reshape(rows, context.shape[1])
    projected = jnp.dot(by_slot, out_weight, preferred_element_type=jnp.float32)
    return (coarse, projected.astype(jnp.bfloat16))


def solution(mesh):
    dp = mesh.shape["dp"]
    seq = mesh.shape["seq"]
    nx = 8 if seq % 8 == 0 else seq
    nz = seq // nx
    grid = Mesh(mesh.devices.reshape(dp, nz, nx), ("dp", "sz", "sx"))
    rows = P(("dp", "sz", "sx"), None)
    return jax.shard_map(
        shards,
        mesh=grid,
        in_specs=(
            rows,
            P(),
            P(None, None, ("sz", "sx")),
            P(),
            P(),
            P(("sz", "sx"), None),
            P(("sz", "sx"), None),
            P(),
            P(("sz", "sx"), None),
        ),
        out_specs=(rows, rows),
        check_vma=False,
    )
```

```python
import jax
import jax.numpy as jnp
from jax import lax
from jax.experimental import pallas as pl
from jax.experimental.pallas import tpu as pltpu
from jax.sharding import Mesh
from jax.sharding import PartitionSpec as P

HEAD_DIM = 128


def normalize(values_in, channel_gain):
    meansq = jnp.mean(values_in * values_in, axis=-1, keepdims=True)
    return values_in * lax.rsqrt(meansq + 1e-06) * channel_gain


def convolve(padded, kernel, row_count):
    summed = jnp.zeros((row_count, kernel[0].shape[1]), jnp.float32)
    for kernel_tap in range(len(kernel)):
        summed = summed + jnp.dot(
            padded[kernel_tap : kernel_tap + row_count],
            kernel[kernel_tap],
            preferred_element_type=jnp.float32,
        )
    return summed


def pool_pairs(levels):
    return jnp.max(levels.reshape(-1, 2, levels.shape[1]), axis=1)


def gather_rows(block):
    inner = lax.all_gather(block, "sx", axis=0, tiled=True)
    return lax.all_gather(inner, "sz", axis=0, tiled=True)


def sx_major(columns, nz, nx, me_z):
    rows = columns.shape[0]
    split = jnp.roll(columns.reshape(rows, nz, nx, -1), -me_z, axis=1)
    return split.transpose(0, 2, 1, 3).reshape(rows, columns.shape[1])


def ring(value, axis, n):
    up = [(i, (i - 1) % n) for i in range(n)]
    down = [(i, (i + 1) % n) for i in range(n)]
    slots = {0: value}
    ahead = behind = value
    for step in range(1, n // 2 + 1):
        ahead = lax.ppermute(ahead, axis, up)
        if step <= (n - 1) // 2:
            behind = lax.ppermute(behind, axis, down)
            ahead, behind = lax.optimization_barrier((ahead, behind))
            slots[(-step) % n] = behind
        else:
            ahead = lax.optimization_barrier(ahead)
        slots[step % n] = ahead
    return [slots[k] for k in range(n)]


def head_kernel(scale_ref, q_ref, k_ref, v_ref, o_ref):
    head = pl.program_id(0)
    scores = lax.dot_general(
        q_ref[...], k_ref[...], (((1,), (1,)), ((), ())), preferred_element_type=jnp.float32
    )
    scores = scores * scale_ref[head] * HEAD_DIM ** (-0.5)
    biggest = jnp.max(scores, axis=1, keepdims=True)
    expon = jnp.exp(scores - biggest)
    total = jnp.sum(expon, axis=1, keepdims=True)
    context = jnp.dot(expon.astype(jnp.bfloat16), v_ref[...], preferred_element_type=jnp.float32)
    o_ref[...] = (context / total).astype(o_ref.dtype)


def attend(queries, key_block, scales):
    row_count = queries.shape[0]
    head_count = scales.shape[0]
    key_count = key_block.shape[0]
    flops = 4 * head_count * row_count * key_count * HEAD_DIM
    return pl.pallas_call(
        head_kernel,
        grid=(head_count,),
        in_specs=[
            pl.BlockSpec(memory_space=pltpu.SMEM),
            pl.BlockSpec((row_count, HEAD_DIM), lambda h: (0, h)),
            pl.BlockSpec((key_count, HEAD_DIM), lambda h: (0, 0)),
            pl.BlockSpec((key_count, HEAD_DIM), lambda h: (0, 1)),
        ],
        out_specs=pl.BlockSpec((row_count, HEAD_DIM), lambda h: (0, h)),
        out_shape=jax.ShapeDtypeStruct((row_count, head_count * HEAD_DIM), jnp.bfloat16),
        cost_estimate=pl.CostEstimate(
            flops=flops,
            transcendentals=head_count * row_count * key_count,
            bytes_accessed=2 * key_block.size + 4 * queries.size,
        ),
    )(scales, queries, key_block, key_block)


def shards(
    features,
    norm_gain,
    conv_weight,
    conv_bias,
    attn_gain,
    query_weight,
    keyval_weight,
    head_scale,
    output_weight,
):
    nz = lax.axis_size("sz")
    nx = lax.axis_size("sx")
    me_x = lax.axis_index("sx")
    rows_here = features.shape[0]
    taps, _, width = conv_weight.shape
    ch_out = conv_bias.shape[0]

    me_z = lax.axis_index("sz")
    normed = jax.nn.gelu(normalize(features.astype(jnp.float32), norm_gain)).astype(jnp.bfloat16)
    plane = lax.all_gather(normed, "sx", axis=0, tiled=True)

    q_cols = query_weight.shape[1]
    lane = 256
    proj_piece = jnp.concatenate([query_weight, keyval_weight], axis=1)
    proj_n = proj_piece.size // lane
    both = jnp.concatenate(
        [proj_piece.reshape(proj_n, lane), output_weight.reshape(-1, lane)], axis=0
    )
    slots = ring((conv_weight, both), "sz", nz)
    kernel = [jnp.concatenate([s[0][tap] for s in slots], axis=1) for tap in range(taps)]
    both_z = jnp.stack([s[1] for s in slots])
    proj_z = both_z[:, :proj_n].reshape(nz * proj_piece.shape[0], proj_piece.shape[1])
    out_z = both_z[:, proj_n:].reshape(nz * output_weight.shape[0], output_weight.shape[1])
    proj_weight = lax.all_gather(proj_z, "sx", axis=0, tiled=True)

    plane_rows = plane.shape[0]
    forward = [(i, i + 1) for i in range(nz - 1)]
    backward = [(i + 1, i) for i in range(nz - 1)]
    low = lax.ppermute(plane[plane_rows - 2 :], "sz", forward)
    high = lax.ppermute(plane[:2], "sz", backward)
    padded = jnp.concatenate([low, plane, high], axis=0)

    bias_all = conv_bias.reshape(nz, nx, width).transpose(1, 0, 2)
    bias = lax.dynamic_index_in_dim(bias_all, me_x, axis=0, keepdims=False)
    bias = jnp.roll(bias, -me_z, axis=0).reshape(nz * width)
    levels = convolve(padded, kernel, plane_rows) + bias[None, :]
    pooled = pool_pairs(levels).astype(jnp.bfloat16)

    coarse_rows = rows_here // 2
    pieces = pooled.reshape(nx, coarse_rows, nz * width)
    received = lax.all_to_all(pieces, "sx", 0, 0, tiled=False)
    received = jnp.roll(received.reshape(nx, coarse_rows, nz, width), me_z, axis=2)
    coarse = received.transpose(1, 2, 0, 3).reshape(coarse_rows, ch_out)

    attn_in = normalize(coarse.astype(jnp.float32), attn_gain).astype(jnp.bfloat16)
    proj = jnp.dot(sx_major(attn_in, nz, nx, me_z), proj_weight, preferred_element_type=jnp.float32)
    queries = proj[:, :q_cols].astype(jnp.bfloat16)
    keyvals = proj[:, q_cols:].astype(jnp.bfloat16)
    kv_plane = lax.all_gather(keyvals, "sx", axis=0, tiled=True)
    kv_plane, out_z = lax.optimization_barrier((kv_plane, out_z))
    key_block = lax.all_gather(kv_plane, "sz", axis=0, tiled=True)
    out_weight = jnp.concatenate(ring(out_z, "sx", nx), axis=0)
    context = attend(queries, key_block, head_scale)
    rows = context.shape[0]
    by_slot = jnp.roll(context.reshape(rows, nz, nx, -1), (-me_z, -me_x), axis=(1, 2))
    by_slot = by_slot.transpose(0, 2, 1, 3).reshape(rows, context.shape[1])
    projected = jnp.dot(by_slot, out_weight, preferred_element_type=jnp.float32)
    return (coarse, projected.astype(jnp.bfloat16))


def solution(mesh):
    dp = mesh.shape["dp"]
    seq = mesh.shape["seq"]
    nx = 8 if seq % 8 == 0 else seq
    nz = seq // nx
    grid = Mesh(mesh.devices.reshape(dp, nz, nx), ("dp", "sz", "sx"))
    rows = P(("dp", "sz", "sx"), None)
    return jax.shard_map(
        shards,
        mesh=grid,
        in_specs=(
            rows,
            P(),
            P(None, None, ("sz", "sx")),
            P(),
            P(),
            P(("sz", "sx"), None),
            P(("sz", "sx"), None),
            P(),
            P(("sz", "sx"), None),
        ),
        out_specs=(rows, rows),
        check_vma=False,
    )
```

```python
import jax
import jax.numpy as jnp
from jax import lax
from jax.experimental import pallas as pl
from jax.experimental.pallas import tpu as pltpu
from jax.sharding import Mesh
from jax.sharding import PartitionSpec as P

HEAD_DIM = 128


def normalize(values_in, channel_gain):
    meansq = jnp.mean(values_in * values_in, axis=-1, keepdims=True)
    return values_in * lax.rsqrt(meansq + 1e-06) * channel_gain


def convolve(padded, kernel, row_count):
    summed = jnp.zeros((row_count, kernel[0].shape[1]), jnp.float32)
    for kernel_tap in range(len(kernel)):
        summed = summed + jnp.dot(
            padded[kernel_tap : kernel_tap + row_count],
            kernel[kernel_tap],
            preferred_element_type=jnp.float32,
        )
    return summed


def pool_pairs(levels):
    return jnp.maximum(levels[0::2], levels[1::2])


def gather_rows(block):
    inner = lax.all_gather(block, "sx", axis=0, tiled=True)
    return lax.all_gather(inner, "sz", axis=0, tiled=True)


def sx_major(columns, nz, nx, me_z):
    rows = columns.shape[0]
    split = jnp.roll(columns.reshape(rows, nz, nx, -1), -me_z, axis=1)
    return split.transpose(0, 2, 1, 3).reshape(rows, columns.shape[1])


def ring(value, axis, n):
    up = [(i, (i - 1) % n) for i in range(n)]
    down = [(i, (i + 1) % n) for i in range(n)]
    slots = {0: value}
    ahead = behind = value
    for step in range(1, n // 2 + 1):
        ahead = lax.ppermute(ahead, axis, up)
        if step <= (n - 1) // 2:
            behind = lax.ppermute(behind, axis, down)
            ahead, behind = lax.optimization_barrier((ahead, behind))
            slots[(-step) % n] = behind
        else:
            ahead = lax.optimization_barrier(ahead)
        slots[step % n] = ahead
    return [slots[k] for k in range(n)]


def head_kernel(scale_ref, q_ref, k_ref, v_ref, o_ref):
    head = pl.program_id(0)
    scores = lax.dot_general(
        q_ref[...], k_ref[...], (((1,), (1,)), ((), ())), preferred_element_type=jnp.float32
    )
    scores = scores * scale_ref[head] * HEAD_DIM ** (-0.5)
    biggest = jnp.max(scores, axis=1, keepdims=True)
    expon = jnp.exp(scores - biggest)
    total = jnp.sum(expon, axis=1, keepdims=True)
    context = jnp.dot(expon.astype(jnp.bfloat16), v_ref[...], preferred_element_type=jnp.float32)
    o_ref[...] = (context / total).astype(o_ref.dtype)


def attend(queries, key_block, scales):
    row_count = queries.shape[0]
    head_count = scales.shape[0]
    key_count = key_block.shape[0]
    flops = 4 * head_count * row_count * key_count * HEAD_DIM
    return pl.pallas_call(
        head_kernel,
        grid=(head_count,),
        in_specs=[
            pl.BlockSpec(memory_space=pltpu.SMEM),
            pl.BlockSpec((row_count, HEAD_DIM), lambda h: (0, h)),
            pl.BlockSpec((key_count, HEAD_DIM), lambda h: (0, 0)),
            pl.BlockSpec((key_count, HEAD_DIM), lambda h: (0, 1)),
        ],
        out_specs=pl.BlockSpec((row_count, HEAD_DIM), lambda h: (0, h)),
        out_shape=jax.ShapeDtypeStruct((row_count, head_count * HEAD_DIM), jnp.bfloat16),
        cost_estimate=pl.CostEstimate(
            flops=flops,
            transcendentals=head_count * row_count * key_count,
            bytes_accessed=2 * key_block.size + 4 * queries.size,
        ),
    )(scales, queries, key_block, key_block)


def shards(
    features,
    norm_gain,
    conv_weight,
    conv_bias,
    attn_gain,
    query_weight,
    keyval_weight,
    head_scale,
    output_weight,
):
    nz = lax.axis_size("sz")
    nx = lax.axis_size("sx")
    me_x = lax.axis_index("sx")
    rows_here = features.shape[0]
    taps, _, width = conv_weight.shape
    ch_out = conv_bias.shape[0]

    me_z = lax.axis_index("sz")
    normed = jax.nn.gelu(normalize(features.astype(jnp.float32), norm_gain)).astype(jnp.bfloat16)
    plane = lax.all_gather(normed, "sx", axis=0, tiled=True)

    q_cols = query_weight.shape[1]
    lane = 256
    proj_piece = jnp.concatenate([query_weight, keyval_weight], axis=1)
    proj_n = proj_piece.size // lane
    both = jnp.concatenate(
        [proj_piece.reshape(proj_n, lane), output_weight.reshape(-1, lane)], axis=0
    )
    slots = ring((conv_weight, both), "sz", nz)
    kernel = [jnp.concatenate([s[0][tap] for s in slots], axis=1) for tap in range(taps)]
    both_z = jnp.stack([s[1] for s in slots])
    proj_z = both_z[:, :proj_n].reshape(nz * proj_piece.shape[0], proj_piece.shape[1])
    out_z = both_z[:, proj_n:].reshape(nz * output_weight.shape[0], output_weight.shape[1])
    proj_weight = lax.all_gather(proj_z, "sx", axis=0, tiled=True)

    plane_rows = plane.shape[0]
    forward = [(i, i + 1) for i in range(nz - 1)]
    backward = [(i + 1, i) for i in range(nz - 1)]
    low = lax.ppermute(plane[plane_rows - 2 :], "sz", forward)
    high = lax.ppermute(plane[:2], "sz", backward)
    padded = jnp.concatenate([low, plane, high], axis=0)

    bias_all = conv_bias.reshape(nz, nx, width).transpose(1, 0, 2)
    bias = lax.dynamic_index_in_dim(bias_all, me_x, axis=0, keepdims=False)
    bias = jnp.roll(bias, -me_z, axis=0).reshape(nz * width)
    levels = convolve(padded, kernel, plane_rows) + bias[None, :]
    pooled = pool_pairs(levels).astype(jnp.bfloat16)

    coarse_rows = rows_here // 2
    pieces = pooled.reshape(nx, coarse_rows, nz * width)
    received = lax.all_to_all(pieces, "sx", 0, 0, tiled=False)
    received = jnp.roll(received.reshape(nx, coarse_rows, nz, width), me_z, axis=2)
    coarse = received.transpose(1, 2, 0, 3).reshape(coarse_rows, ch_out)

    attn_in = normalize(coarse.astype(jnp.float32), attn_gain).astype(jnp.bfloat16)
    proj = jnp.dot(sx_major(attn_in, nz, nx, me_z), proj_weight, preferred_element_type=jnp.float32)
    queries = proj[:, :q_cols].astype(jnp.bfloat16)
    keyvals = proj[:, q_cols:].astype(jnp.bfloat16)
    kv_plane = lax.all_gather(keyvals, "sx", axis=0, tiled=True)
    kv_plane, out_z = lax.optimization_barrier((kv_plane, out_z))
    key_block = lax.all_gather(kv_plane, "sz", axis=0, tiled=True)
    out_weight = jnp.concatenate(ring(out_z, "sx", nx), axis=0)
    context = attend(queries, key_block, head_scale)
    rows = context.shape[0]
    by_slot = jnp.roll(context.reshape(rows, nz, nx, -1), (-me_z, -me_x), axis=(1, 2))
    by_slot = by_slot.transpose(0, 2, 1, 3).reshape(rows, context.shape[1])
    projected = jnp.dot(by_slot, out_weight, preferred_element_type=jnp.float32)
    return (coarse, projected.astype(jnp.bfloat16))


def solution(mesh):
    dp = mesh.shape["dp"]
    seq = mesh.shape["seq"]
    nx = 8 if seq % 8 == 0 else seq
    nz = seq // nx
    grid = Mesh(mesh.devices.reshape(dp, nz, nx), ("dp", "sz", "sx"))
    rows = P(("dp", "sz", "sx"), None)
    return jax.shard_map(
        shards,
        mesh=grid,
        in_specs=(
            rows,
            P(),
            P(None, None, ("sz", "sx")),
            P(),
            P(),
            P(("sz", "sx"), None),
            P(("sz", "sx"), None),
            P(),
            P(("sz", "sx"), None),
        ),
        out_specs=(rows, rows),
        check_vma=False,
    )
```

```python
import jax
import jax.numpy as jnp
from jax import lax
from jax.experimental import pallas as pl
from jax.experimental.pallas import tpu as pltpu
from jax.sharding import Mesh
from jax.sharding import PartitionSpec as P

HEAD_DIM = 128


def normalize(values_in, channel_gain):
    meansq = jnp.mean(values_in * values_in, axis=-1, keepdims=True)
    return values_in * lax.rsqrt(meansq + 1e-06) * channel_gain


def convolve(padded, kernel, row_count):
    summed = jnp.zeros((row_count, kernel[0].shape[1]), jnp.float32)
    for kernel_tap in range(len(kernel)):
        summed = summed + jnp.dot(
            padded[kernel_tap : kernel_tap + row_count],
            kernel[kernel_tap],
            preferred_element_type=jnp.float32,
        )
    return summed


def pool_pairs(levels):
    return jnp.max(levels.reshape(-1, 2, levels.shape[1]), axis=1)


def gather_rows(block):
    inner = lax.all_gather(block, "sx", axis=0, tiled=True)
    return lax.all_gather(inner, "sz", axis=0, tiled=True)


def sx_major(columns, nz, nx, me_z):
    rows = columns.shape[0]
    split = jnp.roll(columns.reshape(rows, nz, nx, -1), -me_z, axis=1)
    return split.transpose(0, 2, 1, 3).reshape(rows, columns.shape[1])


def ring(value, axis, n):
    up = [(i, (i - 1) % n) for i in range(n)]
    down = [(i, (i + 1) % n) for i in range(n)]
    slots = {0: value}
    ahead = behind = value
    for step in range(1, n // 2 + 1):
        ahead = lax.ppermute(ahead, axis, up)
        if step <= (n - 1) // 2:
            behind = lax.ppermute(behind, axis, down)
            ahead, behind = lax.optimization_barrier((ahead, behind))
            slots[(-step) % n] = behind
        else:
            ahead = lax.optimization_barrier(ahead)
        slots[step % n] = ahead
    return [slots[k] for k in range(n)]


def head_kernel(scale_ref, q_ref, k_ref, v_ref, o_ref):
    pair = pl.program_id(0)
    for inner in range(2):
        head = pair * 2 + inner
        cols = slice(inner * HEAD_DIM, (inner + 1) * HEAD_DIM)
        scores = lax.dot_general(
            q_ref[:, cols], k_ref[...], (((1,), (1,)), ((), ())), preferred_element_type=jnp.float32
        )
        scores = scores * scale_ref[head] * HEAD_DIM ** (-0.5)
        biggest = jnp.max(scores, axis=1, keepdims=True)
        expon = jnp.exp(scores - biggest)
        total = jnp.sum(expon, axis=1, keepdims=True)
        context = jnp.dot(expon.astype(jnp.bfloat16), v_ref[...], preferred_element_type=jnp.float32)
        o_ref[:, cols] = (context / total).astype(o_ref.dtype)


def attend(queries, key_block, scales):
    row_count = queries.shape[0]
    head_count = scales.shape[0]
    key_count = key_block.shape[0]
    flops = 4 * head_count * row_count * key_count * HEAD_DIM
    return pl.pallas_call(
        head_kernel,
        grid=(head_count // 2,),
        in_specs=[
            pl.BlockSpec(memory_space=pltpu.SMEM),
            pl.BlockSpec((row_count, 2 * HEAD_DIM), lambda h: (0, h)),
            pl.BlockSpec((key_count, HEAD_DIM), lambda h: (0, 0)),
            pl.BlockSpec((key_count, HEAD_DIM), lambda h: (0, 1)),
        ],
        out_specs=pl.BlockSpec((row_count, 2 * HEAD_DIM), lambda h: (0, h)),
        out_shape=jax.ShapeDtypeStruct((row_count, head_count * HEAD_DIM), jnp.bfloat16),
        cost_estimate=pl.CostEstimate(
            flops=flops,
            transcendentals=head_count * row_count * key_count,
            bytes_accessed=2 * key_block.size + 4 * queries.size,
        ),
    )(scales, queries, key_block, key_block)


def shards(
    features,
    norm_gain,
    conv_weight,
    conv_bias,
    attn_gain,
    query_weight,
    keyval_weight,
    head_scale,
    output_weight,
):
    nz = lax.axis_size("sz")
    nx = lax.axis_size("sx")
    me_x = lax.axis_index("sx")
    rows_here = features.shape[0]
    taps, _, width = conv_weight.shape
    ch_out = conv_bias.shape[0]

    me_z = lax.axis_index("sz")
    normed = jax.nn.gelu(normalize(features.astype(jnp.float32), norm_gain)).astype(jnp.bfloat16)
    plane = lax.all_gather(normed, "sx", axis=0, tiled=True)

    q_cols = query_weight.shape[1]
    lane = 256
    proj_piece = jnp.concatenate([query_weight, keyval_weight], axis=1)
    proj_n = proj_piece.size // lane
    both = jnp.concatenate(
        [proj_piece.reshape(proj_n, lane), output_weight.reshape(-1, lane)], axis=0
    )
    slots = ring((conv_weight, both), "sz", nz)
    kernel = [jnp.concatenate([s[0][tap] for s in slots], axis=1) for tap in range(taps)]
    both_z = jnp.stack([s[1] for s in slots])
    proj_z = both_z[:, :proj_n].reshape(nz * proj_piece.shape[0], proj_piece.shape[1])
    out_z = both_z[:, proj_n:].reshape(nz * output_weight.shape[0], output_weight.shape[1])
    proj_weight = lax.all_gather(proj_z, "sx", axis=0, tiled=True)

    plane_rows = plane.shape[0]
    forward = [(i, i + 1) for i in range(nz - 1)]
    backward = [(i + 1, i) for i in range(nz - 1)]
    low = lax.ppermute(plane[plane_rows - 2 :], "sz", forward)
    high = lax.ppermute(plane[:2], "sz", backward)
    padded = jnp.concatenate([low, plane, high], axis=0)

    bias_all = conv_bias.reshape(nz, nx, width).transpose(1, 0, 2)
    bias = lax.dynamic_index_in_dim(bias_all, me_x, axis=0, keepdims=False)
    bias = jnp.roll(bias, -me_z, axis=0).reshape(nz * width)
    levels = convolve(padded, kernel, plane_rows) + bias[None, :]
    pooled = pool_pairs(levels).astype(jnp.bfloat16)

    coarse_rows = rows_here // 2
    pieces = pooled.reshape(nx, coarse_rows, nz * width)
    received = lax.all_to_all(pieces, "sx", 0, 0, tiled=False)
    received = jnp.roll(received.reshape(nx, coarse_rows, nz, width), me_z, axis=2)
    coarse = received.transpose(1, 2, 0, 3).reshape(coarse_rows, ch_out)

    attn_in = normalize(coarse.astype(jnp.float32), attn_gain).astype(jnp.bfloat16)
    proj = jnp.dot(sx_major(attn_in, nz, nx, me_z), proj_weight, preferred_element_type=jnp.float32)
    queries = proj[:, :q_cols].astype(jnp.bfloat16)
    keyvals = proj[:, q_cols:].astype(jnp.bfloat16)
    kv_plane = lax.all_gather(keyvals, "sx", axis=0, tiled=True)
    kv_plane, out_z = lax.optimization_barrier((kv_plane, out_z))
    key_block = lax.all_gather(kv_plane, "sz", axis=0, tiled=True)
    out_weight = jnp.concatenate(ring(out_z, "sx", nx), axis=0)
    context = attend(queries, key_block, head_scale)
    rows = context.shape[0]
    by_slot = jnp.roll(context.reshape(rows, nz, nx, -1), (-me_z, -me_x), axis=(1, 2))
    by_slot = by_slot.transpose(0, 2, 1, 3).reshape(rows, context.shape[1])
    projected = jnp.dot(by_slot, out_weight, preferred_element_type=jnp.float32)
    return (coarse, projected.astype(jnp.bfloat16))


def solution(mesh):
    dp = mesh.shape["dp"]
    seq = mesh.shape["seq"]
    nx = 8 if seq % 8 == 0 else seq
    nz = seq // nx
    grid = Mesh(mesh.devices.reshape(dp, nz, nx), ("dp", "sz", "sx"))
    rows = P(("dp", "sz", "sx"), None)
    return jax.shard_map(
        shards,
        mesh=grid,
        in_specs=(
            rows,
            P(),
            P(None, None, ("sz", "sx")),
            P(),
            P(),
            P(("sz", "sx"), None),
            P(("sz", "sx"), None),
            P(),
            P(("sz", "sx"), None),
        ),
        out_specs=(rows, rows),
        check_vma=False,
    )
```

```python
import jax
import jax.numpy as jnp
from jax import lax
from jax.experimental import pallas as pl
from jax.experimental.pallas import tpu as pltpu
from jax.sharding import Mesh
from jax.sharding import PartitionSpec as P

HEAD_DIM = 128


def normalize(values_in, channel_gain):
    meansq = jnp.mean(values_in * values_in, axis=-1, keepdims=True)
    return values_in * lax.rsqrt(meansq + 1e-06) * channel_gain


def convolve(padded, kernel, row_count):
    summed = jnp.zeros((row_count, kernel[0].shape[1]), jnp.float32)
    for kernel_tap in range(len(kernel)):
        summed = summed + jnp.dot(
            padded[kernel_tap : kernel_tap + row_count],
            kernel[kernel_tap],
            preferred_element_type=jnp.float32,
        )
    return summed


def pool_pairs(levels):
    return jnp.max(levels.reshape(-1, 2, levels.shape[1]), axis=1)


def gather_rows(block):
    inner = lax.all_gather(block, "sx", axis=0, tiled=True)
    return lax.all_gather(inner, "sz", axis=0, tiled=True)


def sx_major(columns, nz, nx, me_z):
    rows = columns.shape[0]
    split = jnp.roll(columns.reshape(rows, nz, nx, -1), -me_z, axis=1)
    return split.transpose(0, 2, 1, 3).reshape(rows, columns.shape[1])


def ring(value, axis, n):
    up = [(i, (i - 1) % n) for i in range(n)]
    down = [(i, (i + 1) % n) for i in range(n)]
    slots = {0: value}
    ahead = behind = value
    for step in range(1, n // 2 + 1):
        ahead = lax.ppermute(ahead, axis, up)
        if step <= (n - 1) // 2:
            behind = lax.ppermute(behind, axis, down)
            ahead, behind = lax.optimization_barrier((ahead, behind))
            slots[(-step) % n] = behind
        else:
            ahead = lax.optimization_barrier(ahead)
        slots[step % n] = ahead
    return [slots[k] for k in range(n)]


def head_kernel(scale_ref, q_ref, k_ref, v_ref, o_ref):
    pair = pl.program_id(0)
    for inner in range(2):
        head = pair * 2 + inner
        cols = slice(inner * HEAD_DIM, (inner + 1) * HEAD_DIM)
        scores = lax.dot_general(
            q_ref[:, cols], k_ref[...], (((1,), (1,)), ((), ())), preferred_element_type=jnp.float32
        )
        scores = scores * (scale_ref[head] * HEAD_DIM ** (-0.5))
        biggest = jnp.max(scores, axis=1, keepdims=True)
        expon = jnp.exp(scores - biggest)
        total = jnp.sum(expon, axis=1, keepdims=True)
        context = jnp.dot(expon.astype(jnp.bfloat16), v_ref[...], preferred_element_type=jnp.float32)
        o_ref[:, cols] = (context / total).astype(o_ref.dtype)


def attend(queries, key_block, scales):
    row_count = queries.shape[0]
    head_count = scales.shape[0]
    key_count = key_block.shape[0]
    flops = 4 * head_count * row_count * key_count * HEAD_DIM
    return pl.pallas_call(
        head_kernel,
        grid=(head_count // 2,),
        in_specs=[
            pl.BlockSpec(memory_space=pltpu.SMEM),
            pl.BlockSpec((row_count, 2 * HEAD_DIM), lambda h: (0, h)),
            pl.BlockSpec((key_count, HEAD_DIM), lambda h: (0, 0)),
            pl.BlockSpec((key_count, HEAD_DIM), lambda h: (0, 1)),
        ],
        out_specs=pl.BlockSpec((row_count, 2 * HEAD_DIM), lambda h: (0, h)),
        out_shape=jax.ShapeDtypeStruct((row_count, head_count * HEAD_DIM), jnp.bfloat16),
        cost_estimate=pl.CostEstimate(
            flops=flops,
            transcendentals=head_count * row_count * key_count,
            bytes_accessed=2 * key_block.size + 4 * queries.size,
        ),
    )(scales, queries, key_block, key_block)


def shards(
    features,
    norm_gain,
    conv_weight,
    conv_bias,
    attn_gain,
    query_weight,
    keyval_weight,
    head_scale,
    output_weight,
):
    nz = lax.axis_size("sz")
    nx = lax.axis_size("sx")
    me_x = lax.axis_index("sx")
    rows_here = features.shape[0]
    taps, _, width = conv_weight.shape
    ch_out = conv_bias.shape[0]

    me_z = lax.axis_index("sz")
    normed = jax.nn.gelu(normalize(features.astype(jnp.float32), norm_gain)).astype(jnp.bfloat16)
    plane = lax.all_gather(normed, "sx", axis=0, tiled=True)

    q_cols = query_weight.shape[1]
    lane = 256
    proj_piece = jnp.concatenate([query_weight, keyval_weight], axis=1)
    proj_n = proj_piece.size // lane
    both = jnp.concatenate(
        [proj_piece.reshape(proj_n, lane), output_weight.reshape(-1, lane)], axis=0
    )
    slots = ring((conv_weight, both), "sz", nz)
    kernel = [jnp.concatenate([s[0][tap] for s in slots], axis=1) for tap in range(taps)]
    both_z = jnp.stack([s[1] for s in slots])
    proj_z = both_z[:, :proj_n].reshape(nz * proj_piece.shape[0], proj_piece.shape[1])
    out_z = both_z[:, proj_n:].reshape(nz * output_weight.shape[0], output_weight.shape[1])
    proj_weight = lax.all_gather(proj_z, "sx", axis=0, tiled=True)

    plane_rows = plane.shape[0]
    forward = [(i, i + 1) for i in range(nz - 1)]
    backward = [(i + 1, i) for i in range(nz - 1)]
    low = lax.ppermute(plane[plane_rows - 2 :], "sz", forward)
    high = lax.ppermute(plane[:2], "sz", backward)
    padded = jnp.concatenate([low, plane, high], axis=0)

    bias_all = conv_bias.reshape(nz, nx, width).transpose(1, 0, 2)
    bias = lax.dynamic_index_in_dim(bias_all, me_x, axis=0, keepdims=False)
    bias = jnp.roll(bias, -me_z, axis=0).reshape(nz * width)
    levels = convolve(padded, kernel, plane_rows) + bias[None, :]
    pooled = pool_pairs(levels).astype(jnp.bfloat16)

    coarse_rows = rows_here // 2
    pieces = pooled.reshape(nx, coarse_rows, nz * width)
    received = lax.all_to_all(pieces, "sx", 0, 0, tiled=False)
    received = jnp.roll(received.reshape(nx, coarse_rows, nz, width), me_z, axis=2)
    coarse = received.transpose(1, 2, 0, 3).reshape(coarse_rows, ch_out)

    attn_in = normalize(coarse.astype(jnp.float32), attn_gain).astype(jnp.bfloat16)
    proj = jnp.dot(sx_major(attn_in, nz, nx, me_z), proj_weight, preferred_element_type=jnp.float32)
    queries = proj[:, :q_cols].astype(jnp.bfloat16)
    keyvals = proj[:, q_cols:].astype(jnp.bfloat16)
    kv_plane = lax.all_gather(keyvals, "sx", axis=0, tiled=True)
    kv_plane, out_z = lax.optimization_barrier((kv_plane, out_z))
    key_block = lax.all_gather(kv_plane, "sz", axis=0, tiled=True)
    out_weight = jnp.concatenate(ring(out_z, "sx", nx), axis=0)
    context = attend(queries, key_block, head_scale)
    rows = context.shape[0]
    by_slot = jnp.roll(context.reshape(rows, nz, nx, -1), (-me_z, -me_x), axis=(1, 2))
    by_slot = by_slot.transpose(0, 2, 1, 3).reshape(rows, context.shape[1])
    projected = jnp.dot(by_slot, out_weight, preferred_element_type=jnp.float32)
    return (coarse, projected.astype(jnp.bfloat16))


def solution(mesh):
    dp = mesh.shape["dp"]
    seq = mesh.shape["seq"]
    nx = 8 if seq % 8 == 0 else seq
    nz = seq // nx
    grid = Mesh(mesh.devices.reshape(dp, nz, nx), ("dp", "sz", "sx"))
    rows = P(("dp", "sz", "sx"), None)
    return jax.shard_map(
        shards,
        mesh=grid,
        in_specs=(
            rows,
            P(),
            P(None, None, ("sz", "sx")),
            P(),
            P(),
            P(("sz", "sx"), None),
            P(("sz", "sx"), None),
            P(),
            P(("sz", "sx"), None),
        ),
        out_specs=(rows, rows),
        check_vma=False,
    )
```
